256 devices in a mesh: bank: 64 (over x, z, core), dp: 4 (over y).
Axes of the slice: x: 4, y: 4, z: 8, core: 2. Of those that a mesh axis runs over, the one named last changes fastest.
Arguments:
- event_features: bfloat16 [4096, 16, 128], P(('bank', 'dp')), may hold values from -6 to 6
- event_bins: int32 [4096, 16], P(('bank', 'dp')), may hold values from 0 to 7
- positive: int32 [4096], P(('bank', 'dp')), may hold values from 0 to 131071
- teacher_bank: bfloat16 [131072, 1024], P('bank'), may hold values from -16 to 16
- in_weight: bfloat16 [128, 512], replicated, may hold values from -0.5 to 0.5
- embedding_head_weight: bfloat16 [512, 1024], replicated, may hold values from -1 to 1
- membrane_decay_rate: float32 [512], replicated, may hold values from 0.3 to 0.95
Outputs:
- sample_loss: float32 [4096], P(('bank', 'dp'))
- in_grad: float32 [128, 512], P('bank')
- head_weight_gradient: float32 [512, 1024], P('bank')
The draws below stay inside these ranges and needn't reach their ends.
All inputs are finite; a program needn't handle non-finite values.
Results may differ from the reference program's by a relative error of at most 0.0042.
Values may be sent and summed in bfloat16 or wider, within the bound.
No kernel may reach another device: no remote copies, remote signals or barrier semaphores. Data moves between devices by JAX's collectives and lax.ppermute only.
A program may use at most 64 MiB of HBM per device.

```python
from functools import partial
import jax
import jax.numpy as jnp
from jax import lax

D = 1024
H = 512
C_IN = 128
TIME = 8
EVENTS = 16
B_DEV = 16
BANK_DEV = 2048
BANK = 131072
SAMPLES = 4096
N_BANK = 64
N_DP = 4


loading_spread = 0.35


head_alignment = 0.4


def shared_direction(key):
    return jax.random.normal(jax.random.fold_in(key, 72), (D,), jnp.float32)


def draw_teacher_bank(key, part):
    direction = shared_direction(key)
    loadings = jax.random.normal(jax.random.fold_in(key, 73), (BANK,), jnp.float32) * loading_spread
    aligned = loadings[:, None] * direction[None, :]
    scatter = jax.random.normal(jax.random.fold_in(key, 74), (BANK, D), jnp.float32)
    entries = aligned + scatter
    return jnp.clip(entries, -16.0, 16.0).astype(jnp.bfloat16)


def draw_embedding_head_weight(key, part):
    direction = shared_direction(key)
    strengths = jax.random.uniform(jax.random.fold_in(key, 81), (H,), jnp.float32, 0.0, 2.0)
    shaped = strengths[:, None] * direction[None, :] * (head_alignment / H)
    scatter = jax.random.normal(jax.random.fold_in(key, 82), (H, D), jnp.float32)
    values = shaped + scatter * (0.45 / jnp.sqrt(jnp.float32(H)))
    return jnp.clip(values, -1.0, 1.0).astype(jnp.bfloat16)


def plant(array, key, smallest, high):
    spot = [jax.random.randint(jax.random.fold_in(key, axis), (), 0, length) for axis, length in enumerate(array.shape)]
    longest = array.shape.index(max(array.shape))
    beside = spot[:longest] + [(spot[longest] + 1) % array.shape[longest]] + spot[longest + 1:]
    return array.at[tuple(spot)].set(smallest).at[tuple(beside)].set(high)


def steps_of(rng, shape, pieces, low, top_value):
    loudness = 1.0
    for dim, shards_of in pieces:
        heights = jax.random.uniform(jax.random.fold_in(jax.random.fold_in(rng, 6), dim), (shards_of,), jnp.float32, low / len(pieces), top_value / len(pieces))
        loudness = loudness * jnp.repeat(jnp.exp(heights), shape[dim] // shards_of).reshape((-1,) + (1,) * (len(shape) - 1 - dim))
    return loudness


def centred(stream_key, shape, width, bound, shards=(), kind=jnp.bfloat16):
    level = steps_of(stream_key, shape, shards, -0.22, 0.18) if shards else 1.0
    result = jax.random.normal(stream_key, shape, jnp.float32) * width * level
    return jnp.minimum(jnp.maximum(result, -bound), bound).astype(kind)


def setup_inputs(seed: int = 0) -> dict:
    seeds = jax.random.split(jax.random.key(seed), 8)
    return {
        "event_features": centred(seeds[0], (SAMPLES, EVENTS, C_IN), 1.0, 6.0, ((0, 256),)),
        "event_bins": plant(jax.random.randint(seeds[1], (SAMPLES, EVENTS), 0, TIME), jax.random.fold_in(seeds[1], 1), 0, TIME - 1).astype(jnp.int32),
        "positive": plant(jax.random.randint(seeds[2], (SAMPLES,), 0, BANK), jax.random.fold_in(seeds[2], 1), 0, BANK - 1).astype(jnp.int32),
        "teacher_bank": draw_teacher_bank(jax.random.fold_in(seeds[7], 71), 0),
        "in_weight": centred(seeds[4], (C_IN, H), C_IN ** -0.5, 0.5),
        "embedding_head_weight": draw_embedding_head_weight(jax.random.fold_in(seeds[7], 71), 0),
        "membrane_decay_rate": jnp.clip(jax.random.uniform(seeds[6], (H,), jnp.float32, 0.3, 0.95), 0.3, 0.95),
    }


sharpening_divisor = 0.07
objective_divisor = 64.0
threshold = 1.0
sharpness = 4.0
epsilon = 1e-06

def membrane_potential(input_current, membrane_decay_rate):
    potential = jnp.zeros((input_current.shape[0], input_current.shape[2]), jnp.float32)
    spikes = jnp.zeros_like(potential)
    totals = jnp.zeros_like(potential)
    for moment in range(input_current.shape[1]):
        potential = membrane_decay_rate * potential + input_current[:, moment, :] - spikes
        spikes = jax.nn.sigmoid(sharpness * (potential - threshold))
        totals = totals + spikes
    return totals / input_current.shape[1]

def reference(event_features, event_bins, positive, teacher_bank, in_weight, embedding_head_weight, membrane_decay_rate):
    samples = event_features.shape[0]
    onehot = (event_bins[:, None, :] == jnp.arange(TIME, dtype=jnp.int32)[None, :, None]).astype(jnp.float32)
    binned = jnp.einsum('ste,sec->stc', onehot, event_features.astype(jnp.float32)).astype(jnp.bfloat16)
    flat_in = binned.reshape(samples * TIME, C_IN)
    input_current = jnp.dot(flat_in, in_weight, preferred_element_type=jnp.float32).reshape(samples, TIME, H)
    spike_train, leaky_neuron_backward = jax.vjp(partial(membrane_potential, membrane_decay_rate=membrane_decay_rate), input_current)
    spike_train_reduced = spike_train.astype(jnp.bfloat16)
    projected_embedding = jnp.dot(spike_train_reduced, embedding_head_weight, preferred_element_type=jnp.float32)
    length = jnp.sqrt(lax.optimization_barrier(jnp.sum(projected_embedding * projected_embedding, axis=1, keepdims=True)) + epsilon)
    query = projected_embedding / length
    query_low = query.astype(jnp.bfloat16)
    inverse = 1.0 / jnp.sqrt(lax.optimization_barrier(jnp.sum(jnp.square(teacher_bank.astype(jnp.float32)), axis=1)) + epsilon)
    panels = teacher_bank.reshape(N_BANK, BANK_DEV, D)
    inverse_panels = inverse.reshape(N_BANK, BANK_DEV)
    grouped_query = query_low.reshape(N_BANK, N_DP, B_DEV, D)
    grouped_pos = positive.reshape(N_BANK, N_DP, B_DEV)
    loss_parts = []
    derivative_shares = []
    for group_index in range(N_DP):
        student_batch_entries = grouped_query[:, group_index].reshape(N_BANK * B_DEV, D)
        group_pos = grouped_pos[:, group_index].reshape(N_BANK * B_DEV)

        def panel_visit(running, panel_item):
            exponent_total, expected_teacher_vector = running
            teacher_block_matrix, teacher_block_reciprocal = panel_item
            cosine_affinity_matrix = jnp.dot(student_batch_entries, teacher_block_matrix.T, preferred_element_type=jnp.float32) * teacher_block_reciprocal[None, :] / sharpening_divisor
            exponent = jnp.exp(cosine_affinity_matrix)
            weights = (exponent * teacher_block_reciprocal[None, :]).astype(jnp.bfloat16)
            exponent_total = exponent_total + lax.optimization_barrier(jnp.sum(exponent, axis=1))
            expected_teacher_vector = expected_teacher_vector + jnp.dot(weights, teacher_block_matrix, preferred_element_type=jnp.float32)
            return ((exponent_total, expected_teacher_vector), None)
        start_state = (jnp.zeros((N_BANK * B_DEV,), jnp.float32), jnp.zeros((N_BANK * B_DEV, D), jnp.float32))
        (exponent_total, expected_teacher_vector), unused = lax.scan(panel_visit, start_state, (panels, inverse_panels))
        matched_entries = jnp.take(teacher_bank, group_pos, axis=0).astype(jnp.float32)
        matched_reciprocal = jnp.take(inverse, group_pos)
        matched_dot_value = lax.optimization_barrier(jnp.sum(student_batch_entries.astype(jnp.float32) * matched_entries, axis=1)) * matched_reciprocal / sharpening_divisor
        loss_parts.append(jnp.log(exponent_total) - matched_dot_value)
        derivative_shares.append((expected_teacher_vector / exponent_total[:, None] - matched_entries * matched_reciprocal[:, None]) / (sharpening_divisor * objective_divisor))
    sample_loss = jnp.stack(loss_parts).reshape(N_DP, N_BANK, B_DEV).transpose(1, 0, 2).reshape(samples)
    query_grad = jnp.stack(derivative_shares).reshape(N_DP, N_BANK, B_DEV, D).transpose(1, 0, 2, 3).reshape(samples, D)
    projection_gradient = ((query_grad - query * lax.optimization_barrier(jnp.sum(query * query_grad, axis=1, keepdims=True))) / length).astype(jnp.bfloat16)
    head_weight_gradient = jnp.dot(spike_train_reduced.T, projection_gradient, preferred_element_type=jnp.float32)
    spike_train_gradient = jnp.dot(projection_gradient, embedding_head_weight.T, preferred_element_type=jnp.float32)
    input_current_gradient, = leaky_neuron_backward(spike_train_gradient)
    current_low = input_current_gradient.astype(jnp.bfloat16).reshape(samples * TIME, H)
    in_grad = jnp.dot(flat_in.T, current_low, preferred_element_type=jnp.float32)
    return (sample_loss, in_grad, head_weight_gradient)
```

```python
from functools import partial

import jax
import jax.numpy as jnp
from jax import lax
from jax.sharding import Mesh
from jax.sharding import PartitionSpec as P

D = 1024
H = 512
C_IN = 128
TIME = 8


sharpening_divisor = 0.07
objective_divisor = 64.0
threshold = 1.0
sharpness = 4.0
epsilon = 1e-06

BANK_AXES = ("bx", "bz", "bc")
SAMPLE_AXES = ("bx", "bz", "bc", "dp")
GATHER_ORDER = ("bx", "bz", "bc")
CODE_COLS = 128


def membrane_potential(input_current, membrane_decay_rate):
    potential = jnp.zeros((input_current.shape[0], input_current.shape[2]), jnp.float32)
    spikes = jnp.zeros_like(potential)
    totals = jnp.zeros_like(potential)
    for moment in range(input_current.shape[1]):
        potential = membrane_decay_rate * potential + input_current[:, moment, :] - spikes
        spikes = jax.nn.sigmoid(sharpness * (potential - threshold))
        totals = totals + spikes
    return totals / input_current.shape[1]


def gathered_block_index():
    index = 0
    for name in reversed(GATHER_ORDER):
        index = index * lax.axis_size(name) + lax.axis_index(name)
    return index


def bank_index():
    index = 0
    for name in BANK_AXES:
        index = index * lax.axis_size(name) + lax.axis_index(name)
    return index


def body(
    event_features,
    event_bins,
    positive,
    teacher_bank,
    in_weight,
    embedding_head_weight,
    membrane_decay_rate,
):
    per_device = positive.shape[0]
    bank_rows = teacher_bank.shape[0]
    onehot = (event_bins[:, None, :] == jnp.arange(TIME, dtype=jnp.int32)[None, :, None]).astype(
        jnp.bfloat16
    )
    binned = jnp.einsum(
        "ste,sec->stc", onehot, event_features, preferred_element_type=jnp.float32
    ).astype(jnp.bfloat16)
    flat_in = binned.reshape(per_device * TIME, C_IN)
    input_current = jnp.dot(flat_in, in_weight, preferred_element_type=jnp.float32).reshape(
        per_device, TIME, H
    )
    spike_train, leaky_neuron_backward = jax.vjp(
        partial(membrane_potential, membrane_decay_rate=membrane_decay_rate), input_current
    )
    spike_train_reduced = spike_train.astype(jnp.bfloat16)
    projected_embedding = jnp.dot(
        spike_train_reduced, embedding_head_weight, preferred_element_type=jnp.float32
    )
    length = jnp.sqrt(
        jnp.sum(projected_embedding * projected_embedding, axis=1, keepdims=True) + epsilon
    )
    query = projected_embedding / length
    query_low = query.astype(jnp.bfloat16)

    digits = jnp.stack([(positive >> 12) & 63, (positive >> 6) & 63, positive & 63], axis=1)
    code = jnp.zeros((per_device, CODE_COLS), jnp.bfloat16).at[:, :3].set(
        digits.astype(jnp.bfloat16)
    )
    gathered = jnp.concatenate([query_low, code], axis=1)
    for name in GATHER_ORDER:
        gathered = lax.all_gather(gathered, name, axis=0, tiled=True)
    gathered_query = gathered[:, :D]
    gathered_digits = gathered[:, D : D + 3].astype(jnp.int32)
    gathered_pos = (
        gathered_digits[:, 0] * 4096 + gathered_digits[:, 1] * 64 + gathered_digits[:, 2]
    )

    start_row = bank_index() * bank_rows
    inverse = 1.0 / jnp.sqrt(
        jnp.sum(jnp.square(teacher_bank.astype(jnp.float32)), axis=1) + epsilon
    )
    local_index = gathered_pos - start_row
    is_owner = (local_index >= 0) & (local_index < bank_rows)
    local_index = jnp.clip(local_index, 0, bank_rows - 1)

    cosine_affinity_matrix = (
        jnp.dot(gathered_query, teacher_bank.T, preferred_element_type=jnp.float32)
        * inverse[None, :]
        / sharpening_divisor
    )
    exponent = jnp.exp(cosine_affinity_matrix)
    weights = (exponent * inverse[None, :]).astype(jnp.bfloat16)
    partition_part = jnp.sum(exponent, axis=1)
    column = lax.broadcasted_iota(jnp.int32, cosine_affinity_matrix.shape, 1)
    picked = jnp.sum(
        jnp.where(column == local_index[:, None], cosine_affinity_matrix, 0.0), axis=1
    )
    pos_part = jnp.where(is_owner, picked, 0.0)

    stats = jnp.stack([partition_part, pos_part])
    for name in reversed(GATHER_ORDER):
        stats = lax.psum(stats, name)
    exponent_total = stats[0]
    matched_dot_value = stats[1]
    own_start = gathered_block_index() * per_device
    own_partition = lax.dynamic_slice_in_dim(exponent_total, own_start, per_device, 0)
    own_pos = lax.dynamic_slice_in_dim(matched_dot_value, own_start, per_device, 0)
    sample_loss = jnp.log(own_partition) - own_pos

    partial_sums = jnp.dot(weights, teacher_bank, preferred_element_type=jnp.float32)
    matched_entries = (
        jnp.take(teacher_bank, local_index, axis=0).astype(jnp.float32)
        * jnp.take(inverse, local_index)[:, None]
    )
    local_owned_rows = jnp.where(is_owner[:, None], matched_entries, 0.0)
    query_grad = (partial_sums / exponent_total[:, None] - local_owned_rows) / (
        sharpening_divisor * objective_divisor
    )
    for name in reversed(GATHER_ORDER):
        query_grad = lax.psum_scatter(query_grad, name, scatter_dimension=0, tiled=True)

    projection_gradient = (
        (query_grad - query * jnp.sum(query * query_grad, axis=1, keepdims=True)) / length
    ).astype(jnp.bfloat16)
    head_weight_piece = jnp.dot(
        spike_train_reduced.T, projection_gradient, preferred_element_type=jnp.float32
    )
    spike_train_gradient = jnp.dot(
        projection_gradient, embedding_head_weight.T, preferred_element_type=jnp.float32
    )
    (input_current_gradient,) = leaky_neuron_backward(spike_train_gradient)
    current_low = input_current_gradient.astype(jnp.bfloat16).reshape(per_device * TIME, H)
    in_part = jnp.dot(flat_in.T, current_low, preferred_element_type=jnp.float32)

    sizes = [lax.axis_size(name) for name in BANK_AXES]
    bank_size = sizes[0] * sizes[1] * sizes[2]
    in_share_rows = C_IN // bank_size
    head_share_rows = H // bank_size
    grads = jnp.concatenate(
        [
            in_part.reshape(bank_size, in_share_rows * H),
            head_weight_piece.reshape(bank_size, head_share_rows * D),
        ],
        axis=1,
    )
    order = [BANK_AXES.index(name) for name in reversed(GATHER_ORDER)]
    grads = (
        grads.reshape(*sizes, grads.shape[1])
        .transpose(*order, 3)
        .reshape(bank_size, grads.shape[1])
    )
    for name in reversed(GATHER_ORDER):
        grads = lax.psum_scatter(grads, name, scatter_dimension=0, tiled=True)
    grads = lax.psum(grads, "dp")
    in_grad = grads[0, : in_share_rows * H].reshape(in_share_rows, H)
    head_weight_gradient = grads[0, in_share_rows * H :].reshape(head_share_rows, D)
    return (sample_loss, in_grad, head_weight_gradient)


def split_mesh(mesh):
    devices = mesh.devices
    column = devices[:, 0]
    try:
        xs = sorted({int(d.coords[0]) for d in column})
        zs = sorted({int(d.coords[2]) for d in column})
        cs = sorted({int(d.core_on_chip) for d in column})
        nx, nz, nc = len(xs), len(zs), len(cs)
        ok = nx * nz * nc == column.shape[0]
        for b, d in enumerate(column):
            want = (b // (nz * nc), (b // nc) % nz, b % nc)
            got = (xs.index(int(d.coords[0])), zs.index(int(d.coords[2])), cs.index(int(d.core_on_chip)))
            ok = ok and want == got
    except (AttributeError, IndexError, TypeError):
        ok = False
    if not ok:
        nx, nz, nc = 1, 1, column.shape[0]
    return Mesh(devices.reshape(nx, nz, nc, devices.shape[1]), SAMPLE_AXES)


def solution(mesh):
    split = split_mesh(mesh)
    in_specs = (
        P(SAMPLE_AXES, None, None),
        P(SAMPLE_AXES, None),
        P(SAMPLE_AXES),
        P(BANK_AXES, None),
        P(),
        P(),
        P(),
    )
    out_specs = (P(SAMPLE_AXES), P(BANK_AXES, None), P(BANK_AXES, None))
    return jax.shard_map(body, mesh=split, in_specs=in_specs, out_specs=out_specs, check_vma=False)
```

```python
from functools import partial

import jax
import jax.numpy as jnp
from jax import lax
from jax.sharding import Mesh
from jax.sharding import PartitionSpec as P

D = 1024
H = 512
C_IN = 128
TIME = 8


sharpening_divisor = 0.07
objective_divisor = 64.0
threshold = 1.0
sharpness = 4.0
epsilon = 1e-06

BANK_AXES = ("bx", "bz", "bc")
SAMPLE_AXES = ("bx", "bz", "bc", "dp")
GATHER_ORDER = ("bx", "bz", "bc")
CODE_COLS = 128


def membrane_potential(input_current, membrane_decay_rate):
    potential = jnp.zeros((input_current.shape[0], input_current.shape[2]), jnp.float32)
    spikes = jnp.zeros_like(potential)
    totals = jnp.zeros_like(potential)
    for moment in range(input_current.shape[1]):
        potential = membrane_decay_rate * potential + input_current[:, moment, :] - spikes
        spikes = jax.nn.sigmoid(sharpness * (potential - threshold))
        totals = totals + spikes
    return totals / input_current.shape[1]


def shift_pairs(name, shift):
    size = lax.axis_size(name)
    return [(j, (j + shift) % size) for j in range(size)]


def gather_relative(x, name):
    size = lax.axis_size(name)
    blocks = [x] + [lax.ppermute(x, name, shift_pairs(name, k)) for k in range(1, size)]
    return jnp.concatenate(blocks, axis=0)


def sum_relative(x, name, axis):
    size = lax.axis_size(name)
    total = x
    for k in range(1, size):
        total = total + jnp.roll(lax.ppermute(x, name, shift_pairs(name, k)), k, axis=axis)
    return total


def sum_all(x, name):
    size = lax.axis_size(name)
    total = x
    for k in range(1, size):
        total = total + lax.ppermute(x, name, shift_pairs(name, k))
    return total


def ring_scatter_sum(pick, name, size):
    if size == 1:
        return pick(0)
    if size == 2:
        return pick(0) + lax.ppermute(pick(1), name, shift_pairs(name, 1))
    half = pick(0).shape[-1] // 2
    ahead = pick(1)[..., :half]
    behind = pick(size - 1)[..., half:]
    for step in range(1, size):
        ahead = lax.ppermute(ahead, name, shift_pairs(name, 1)) + pick((1 + step) % size)[..., :half]
        behind = (
            lax.ppermute(behind, name, shift_pairs(name, -1))
            + pick((size - 1 - step) % size)[..., half:]
        )
    return jnp.concatenate([ahead, behind], axis=-1)


def scatter_relative(x, name):
    size = lax.axis_size(name)
    blocks = x.reshape(size, x.shape[0] // size, *x.shape[1:])
    return ring_scatter_sum(lambda k: blocks[k], name, size)


def scatter_absolute(x, name):
    size = lax.axis_size(name)
    rows = x.shape[0] // size
    me = lax.axis_index(name)

    def pick(k):
        return lax.dynamic_slice_in_dim(x, ((me - k) % size) * rows, rows, 0)

    return ring_scatter_sum(pick, name, size)


def bank_index():
    index = 0
    for name in BANK_AXES:
        index = index * lax.axis_size(name) + lax.axis_index(name)
    return index


def body(
    event_features,
    event_bins,
    positive,
    teacher_bank,
    in_weight,
    embedding_head_weight,
    membrane_decay_rate,
):
    per_device = positive.shape[0]
    bank_rows = teacher_bank.shape[0]
    onehot = (event_bins[:, None, :] == jnp.arange(TIME, dtype=jnp.int32)[None, :, None]).astype(
        jnp.bfloat16
    )
    binned = jnp.einsum(
        "ste,sec->stc", onehot, event_features, preferred_element_type=jnp.float32
    ).astype(jnp.bfloat16)
    flat_in = binned.reshape(per_device * TIME, C_IN)
    input_current = jnp.dot(flat_in, in_weight, preferred_element_type=jnp.float32).reshape(
        per_device, TIME, H
    )
    spike_train, leaky_neuron_backward = jax.vjp(
        partial(membrane_potential, membrane_decay_rate=membrane_decay_rate), input_current
    )
    spike_train_reduced = spike_train.astype(jnp.bfloat16)
    projected_embedding = jnp.dot(
        spike_train_reduced, embedding_head_weight, preferred_element_type=jnp.float32
    )
    length = jnp.sqrt(
        jnp.sum(projected_embedding * projected_embedding, axis=1, keepdims=True) + epsilon
    )
    query = projected_embedding / length
    query_low = query.astype(jnp.bfloat16)

    digits = jnp.stack([(positive >> 12) & 63, (positive >> 6) & 63, positive & 63], axis=1)
    code = jnp.zeros((per_device, CODE_COLS), jnp.bfloat16).at[:, :3].set(
        digits.astype(jnp.bfloat16)
    )
    gathered = jnp.concatenate([query_low, code], axis=1)
    for name in GATHER_ORDER:
        gathered = gather_relative(gathered, name)
    gathered_query = gathered[:, :D]
    gathered_digits = gathered[:, D : D + 3].astype(jnp.int32)
    gathered_pos = (
        gathered_digits[:, 0] * 4096 + gathered_digits[:, 1] * 64 + gathered_digits[:, 2]
    )

    start_row = bank_index() * bank_rows
    inverse = 1.0 / jnp.sqrt(
        jnp.sum(jnp.square(teacher_bank.astype(jnp.float32)), axis=1) + epsilon
    )
    local_index = gathered_pos - start_row
    is_owner = (local_index >= 0) & (local_index < bank_rows)
    local_index = jnp.clip(local_index, 0, bank_rows - 1)

    cosine_affinity_matrix = (
        jnp.dot(gathered_query, teacher_bank.T, preferred_element_type=jnp.float32)
        * inverse[None, :]
        / sharpening_divisor
    )
    exponent = jnp.exp(cosine_affinity_matrix)
    weights = (exponent * inverse[None, :]).astype(jnp.bfloat16)
    partition_part = jnp.sum(exponent, axis=1)
    column = lax.broadcasted_iota(jnp.int32, cosine_affinity_matrix.shape, 1)
    picked = jnp.sum(
        jnp.where(column == local_index[:, None], cosine_affinity_matrix, 0.0), axis=1
    )
    pos_part = jnp.where(is_owner, picked, 0.0)

    layout = list(reversed(GATHER_ORDER))
    stats = jnp.stack([partition_part, pos_part]).reshape(
        2, *[lax.axis_size(name) for name in layout], per_device
    )
    for name in layout:
        stats = sum_relative(stats, name, 1 + layout.index(name))
    stats = stats.reshape(2, -1)
    exponent_total = stats[0]
    matched_dot_value = stats[1]
    own_start = 0
    own_partition = lax.dynamic_slice_in_dim(exponent_total, own_start, per_device, 0)
    own_pos = lax.dynamic_slice_in_dim(matched_dot_value, own_start, per_device, 0)
    sample_loss = jnp.log(own_partition) - own_pos

    partial_sums = jnp.dot(weights, teacher_bank, preferred_element_type=jnp.float32)
    matched_entries = (
        jnp.take(teacher_bank, local_index, axis=0).astype(jnp.float32)
        * jnp.take(inverse, local_index)[:, None]
    )
    local_owned_rows = jnp.where(is_owner[:, None], matched_entries, 0.0)
    query_grad = (partial_sums / exponent_total[:, None] - local_owned_rows) / (
        sharpening_divisor * objective_divisor
    )
    for name in reversed(GATHER_ORDER):
        query_grad = scatter_relative(query_grad, name)

    projection_gradient = (
        (query_grad - query * jnp.sum(query * query_grad, axis=1, keepdims=True)) / length
    ).astype(jnp.bfloat16)
    head_weight_piece = jnp.dot(
        spike_train_reduced.T, projection_gradient, preferred_element_type=jnp.float32
    )
    spike_train_gradient = jnp.dot(
        projection_gradient, embedding_head_weight.T, preferred_element_type=jnp.float32
    )
    (input_current_gradient,) = leaky_neuron_backward(spike_train_gradient)
    current_low = input_current_gradient.astype(jnp.bfloat16).reshape(per_device * TIME, H)
    in_part = jnp.dot(flat_in.T, current_low, preferred_element_type=jnp.float32)

    sizes = [lax.axis_size(name) for name in BANK_AXES]
    bank_size = sizes[0] * sizes[1] * sizes[2]
    in_share_rows = C_IN // bank_size
    head_share_rows = H // bank_size
    grads = jnp.concatenate(
        [
            in_part.reshape(bank_size, in_share_rows * H),
            head_weight_piece.reshape(bank_size, head_share_rows * D),
        ],
        axis=1,
    )
    order = [BANK_AXES.index(name) for name in reversed(GATHER_ORDER)]
    grads = (
        grads.reshape(*sizes, grads.shape[1])
        .transpose(*order, 3)
        .reshape(bank_size, grads.shape[1])
    )
    for name in reversed(GATHER_ORDER):
        grads = scatter_absolute(grads, name)
    grads = sum_all(grads, "dp")
    in_grad = grads[0, : in_share_rows * H].reshape(in_share_rows, H)
    head_weight_gradient = grads[0, in_share_rows * H :].reshape(head_share_rows, D)
    return (sample_loss, in_grad, head_weight_gradient)


def split_mesh(mesh):
    devices = mesh.devices
    column = devices[:, 0]
    try:
        xs = sorted({int(d.coords[0]) for d in column})
        zs = sorted({int(d.coords[2]) for d in column})
        cs = sorted({int(d.core_on_chip) for d in column})
        nx, nz, nc = len(xs), len(zs), len(cs)
        ok = nx * nz * nc == column.shape[0]
        for b, d in enumerate(column):
            want = (b // (nz * nc), (b // nc) % nz, b % nc)
            got = (xs.index(int(d.coords[0])), zs.index(int(d.coords[2])), cs.index(int(d.core_on_chip)))
            ok = ok and want == got
    except (AttributeError, IndexError, TypeError):
        ok = False
    if not ok:
        nx, nz, nc = 1, 1, column.shape[0]
    return Mesh(devices.reshape(nx, nz, nc, devices.shape[1]), SAMPLE_AXES)


def solution(mesh):
    split = split_mesh(mesh)
    in_specs = (
        P(SAMPLE_AXES, None, None),
        P(SAMPLE_AXES, None),
        P(SAMPLE_AXES),
        P(BANK_AXES, None),
        P(),
        P(),
        P(),
    )
    out_specs = (P(SAMPLE_AXES), P(BANK_AXES, None), P(BANK_AXES, None))
    return jax.shard_map(body, mesh=split, in_specs=in_specs, out_specs=out_specs, check_vma=False)
```

```python
from functools import partial

import jax
import jax.numpy as jnp
from jax import lax
from jax.sharding import Mesh
from jax.sharding import PartitionSpec as P

D = 1024
H = 512
C_IN = 128
TIME = 8


sharpening_divisor = 0.07
objective_divisor = 64.0
threshold = 1.0
sharpness = 4.0
epsilon = 1e-06

BANK_AXES = ("bx", "bz", "bc")
SAMPLE_AXES = ("bx", "bz", "bc", "dp")
GATHER_ORDER = ("bx", "bz", "bc")
CODE_COLS = 128


def membrane_potential(input_current, membrane_decay_rate):
    potential = jnp.zeros((input_current.shape[0], input_current.shape[2]), jnp.float32)
    spikes = jnp.zeros_like(potential)
    totals = jnp.zeros_like(potential)
    for moment in range(input_current.shape[1]):
        potential = membrane_decay_rate * potential + input_current[:, moment, :] - spikes
        spikes = jax.nn.sigmoid(sharpness * (potential - threshold))
        totals = totals + spikes
    return totals / input_current.shape[1]


def shift_pairs(name, shift):
    size = lax.axis_size(name)
    return [(j, (j + shift) % size) for j in range(size)]


def gather_relative(x, name):
    size = lax.axis_size(name)
    blocks = [x] + [lax.ppermute(x, name, shift_pairs(name, k)) for k in range(1, size)]
    return jnp.concatenate(blocks, axis=0)


def sum_relative(x, name, axis):
    size = lax.axis_size(name)
    total = x
    for k in range(1, size):
        total = total + jnp.roll(lax.ppermute(x, name, shift_pairs(name, k)), k, axis=axis)
    return total


def sum_all(x, name):
    size = lax.axis_size(name)
    total = x
    for k in range(1, size):
        total = total + lax.ppermute(x, name, shift_pairs(name, k))
    return total


def ring_scatter_sum(pick, name, size):
    total = pick(0)
    for k in range(1, size):
        total = total + lax.ppermute(pick(k), name, shift_pairs(name, -k))
    return total


def scatter_relative(x, name):
    size = lax.axis_size(name)
    blocks = x.reshape(size, x.shape[0] // size, *x.shape[1:])
    return ring_scatter_sum(lambda k: blocks[k], name, size)


def scatter_absolute(x, name):
    size = lax.axis_size(name)
    rows = x.shape[0] // size
    me = lax.axis_index(name)

    def pick(k):
        return lax.dynamic_slice_in_dim(x, ((me - k) % size) * rows, rows, 0)

    return ring_scatter_sum(pick, name, size)


def bank_index():
    index = 0
    for name in BANK_AXES:
        index = index * lax.axis_size(name) + lax.axis_index(name)
    return index


def body(
    event_features,
    event_bins,
    positive,
    teacher_bank,
    in_weight,
    embedding_head_weight,
    membrane_decay_rate,
):
    per_device = positive.shape[0]
    bank_rows = teacher_bank.shape[0]
    onehot = (event_bins[:, None, :] == jnp.arange(TIME, dtype=jnp.int32)[None, :, None]).astype(
        jnp.bfloat16
    )
    binned = jnp.einsum(
        "ste,sec->stc", onehot, event_features, preferred_element_type=jnp.float32
    ).astype(jnp.bfloat16)
    flat_in = binned.reshape(per_device * TIME, C_IN)
    input_current = jnp.dot(flat_in, in_weight, preferred_element_type=jnp.float32).reshape(
        per_device, TIME, H
    )
    spike_train, leaky_neuron_backward = jax.vjp(
        partial(membrane_potential, membrane_decay_rate=membrane_decay_rate), input_current
    )
    spike_train_reduced = spike_train.astype(jnp.bfloat16)
    projected_embedding = jnp.dot(
        spike_train_reduced, embedding_head_weight, preferred_element_type=jnp.float32
    )
    length = jnp.sqrt(
        jnp.sum(projected_embedding * projected_embedding, axis=1, keepdims=True) + epsilon
    )
    query = projected_embedding / length
    query_low = query.astype(jnp.bfloat16)

    digits = jnp.stack([(positive >> 12) & 63, (positive >> 6) & 63, positive & 63], axis=1)
    code = jnp.zeros((per_device, CODE_COLS), jnp.bfloat16).at[:, :3].set(
        digits.astype(jnp.bfloat16)
    )
    gathered = jnp.concatenate([query_low, code], axis=1)
    for name in GATHER_ORDER:
        gathered = gather_relative(gathered, name)
    gathered_query = gathered[:, :D]
    gathered_digits = gathered[:, D : D + 3].astype(jnp.int32)
    gathered_pos = (
        gathered_digits[:, 0] * 4096 + gathered_digits[:, 1] * 64 + gathered_digits[:, 2]
    )

    start_row = bank_index() * bank_rows
    inverse = 1.0 / jnp.sqrt(
        jnp.sum(jnp.square(teacher_bank.astype(jnp.float32)), axis=1) + epsilon
    )
    local_index = gathered_pos - start_row
    is_owner = (local_index >= 0) & (local_index < bank_rows)
    local_index = jnp.clip(local_index, 0, bank_rows - 1)

    cosine_affinity_matrix = (
        jnp.dot(gathered_query, teacher_bank.T, preferred_element_type=jnp.float32)
        * inverse[None, :]
        / sharpening_divisor
    )
    exponent = jnp.exp(cosine_affinity_matrix)
    weights = (exponent * inverse[None, :]).astype(jnp.bfloat16)
    partition_part = jnp.sum(exponent, axis=1)
    column = lax.broadcasted_iota(jnp.int32, cosine_affinity_matrix.shape, 1)
    picked = jnp.sum(
        jnp.where(column == local_index[:, None], cosine_affinity_matrix, 0.0), axis=1
    )
    pos_part = jnp.where(is_owner, picked, 0.0)

    layout = list(reversed(GATHER_ORDER))
    stats = jnp.stack([partition_part, pos_part]).reshape(
        2, *[lax.axis_size(name) for name in layout], per_device
    )
    for name in layout:
        stats = sum_relative(stats, name, 1 + layout.index(name))
    stats = stats.reshape(2, -1)
    exponent_total = stats[0]
    matched_dot_value = stats[1]
    own_start = 0
    own_partition = lax.dynamic_slice_in_dim(exponent_total, own_start, per_device, 0)
    own_pos = lax.dynamic_slice_in_dim(matched_dot_value, own_start, per_device, 0)
    sample_loss = jnp.log(own_partition) - own_pos

    partial_sums = jnp.dot(weights, teacher_bank, preferred_element_type=jnp.float32)
    matched_entries = (
        jnp.take(teacher_bank, local_index, axis=0).astype(jnp.float32)
        * jnp.take(inverse, local_index)[:, None]
    )
    local_owned_rows = jnp.where(is_owner[:, None], matched_entries, 0.0)
    query_grad = (partial_sums / exponent_total[:, None] - local_owned_rows) / (
        sharpening_divisor * objective_divisor
    )
    for name in reversed(GATHER_ORDER):
        query_grad = scatter_relative(query_grad, name)

    projection_gradient = (
        (query_grad - query * jnp.sum(query * query_grad, axis=1, keepdims=True)) / length
    ).astype(jnp.bfloat16)
    head_weight_piece = jnp.dot(
        spike_train_reduced.T, projection_gradient, preferred_element_type=jnp.float32
    )
    spike_train_gradient = jnp.dot(
        projection_gradient, embedding_head_weight.T, preferred_element_type=jnp.float32
    )
    (input_current_gradient,) = leaky_neuron_backward(spike_train_gradient)
    current_low = input_current_gradient.astype(jnp.bfloat16).reshape(per_device * TIME, H)
    in_part = jnp.dot(flat_in.T, current_low, preferred_element_type=jnp.float32)

    sizes = [lax.axis_size(name) for name in BANK_AXES]
    bank_size = sizes[0] * sizes[1] * sizes[2]
    in_share_rows = C_IN // bank_size
    head_share_rows = H // bank_size
    grads = jnp.concatenate(
        [
            in_part.reshape(bank_size, in_share_rows * H),
            head_weight_piece.reshape(bank_size, head_share_rows * D),
        ],
        axis=1,
    )
    order = [BANK_AXES.index(name) for name in reversed(GATHER_ORDER)]
    grads = (
        grads.reshape(*sizes, grads.shape[1])
        .transpose(*order, 3)
        .reshape(bank_size, grads.shape[1])
    )
    for name in reversed(GATHER_ORDER):
        grads = scatter_absolute(grads, name)
    grads = sum_all(grads, "dp")
    in_grad = grads[0, : in_share_rows * H].reshape(in_share_rows, H)
    head_weight_gradient = grads[0, in_share_rows * H :].reshape(head_share_rows, D)
    return (sample_loss, in_grad, head_weight_gradient)


def split_mesh(mesh):
    devices = mesh.devices
    column = devices[:, 0]
    try:
        xs = sorted({int(d.coords[0]) for d in column})
        zs = sorted({int(d.coords[2]) for d in column})
        cs = sorted({int(d.core_on_chip) for d in column})
        nx, nz, nc = len(xs), len(zs), len(cs)
        ok = nx * nz * nc == column.shape[0]
        for b, d in enumerate(column):
            want = (b // (nz * nc), (b // nc) % nz, b % nc)
            got = (xs.index(int(d.coords[0])), zs.index(int(d.coords[2])), cs.index(int(d.core_on_chip)))
            ok = ok and want == got
    except (AttributeError, IndexError, TypeError):
        ok = False
    if not ok:
        nx, nz, nc = 1, 1, column.shape[0]
    return Mesh(devices.reshape(nx, nz, nc, devices.shape[1]), SAMPLE_AXES)


def solution(mesh):
    split = split_mesh(mesh)
    in_specs = (
        P(SAMPLE_AXES, None, None),
        P(SAMPLE_AXES, None),
        P(SAMPLE_AXES),
        P(BANK_AXES, None),
        P(),
        P(),
        P(),
    )
    out_specs = (P(SAMPLE_AXES), P(BANK_AXES, None), P(BANK_AXES, None))
    return jax.shard_map(body, mesh=split, in_specs=in_specs, out_specs=out_specs, check_vma=False)
```

```python
from functools import partial

import jax
import jax.numpy as jnp
from jax import lax
from jax.sharding import Mesh
from jax.sharding import PartitionSpec as P

D = 1024
H = 512
C_IN = 128
TIME = 8


sharpening_divisor = 0.07
objective_divisor = 64.0
threshold = 1.0
sharpness = 4.0
epsilon = 1e-06

BANK_AXES = ("bx", "bz", "bc")
SAMPLE_AXES = ("bx", "bz", "bc", "dp")
GATHER_ORDER = ("bx", "bz", "bc")
CODE_COLS = 128


def membrane_potential(input_current, membrane_decay_rate):
    potential = jnp.zeros((input_current.shape[0], input_current.shape[2]), jnp.float32)
    spikes = jnp.zeros_like(potential)
    totals = jnp.zeros_like(potential)
    for moment in range(input_current.shape[1]):
        potential = membrane_decay_rate * potential + input_current[:, moment, :] - spikes
        spikes = jax.nn.sigmoid(sharpness * (potential - threshold))
        totals = totals + spikes
    return totals / input_current.shape[1]


def shift_pairs(name, shift):
    size = lax.axis_size(name)
    return [(j, (j + shift) % size) for j in range(size)]


def gather_relative(x, name):
    size = lax.axis_size(name)
    blocks = [x] + [lax.ppermute(x, name, shift_pairs(name, k)) for k in range(1, size)]
    return jnp.concatenate(blocks, axis=0)


def sum_relative(x, name, axis):
    size = lax.axis_size(name)
    total = x
    for k in range(1, size):
        total = total + jnp.roll(lax.ppermute(x, name, shift_pairs(name, k)), k, axis=axis)
    return total


def sum_all(x, name):
    size = lax.axis_size(name)
    total = x
    for k in range(1, size):
        total = total + lax.ppermute(x, name, shift_pairs(name, k))
    return total


def ring_scatter_sum(pick, name, size):
    total = pick(0)
    for k in range(1, size):
        total = total + lax.ppermute(pick(k), name, shift_pairs(name, -k))
    return total


def scatter_relative(x, name):
    size = lax.axis_size(name)
    blocks = x.reshape(size, x.shape[0] // size, *x.shape[1:])
    return ring_scatter_sum(lambda k: blocks[k], name, size)


def scatter_absolute(x, name):
    size = lax.axis_size(name)
    rows = x.shape[0] // size
    me = lax.axis_index(name)

    def pick(k):
        return lax.dynamic_slice_in_dim(x, ((me - k) % size) * rows, rows, 0)

    return ring_scatter_sum(pick, name, size)


def scatter_two_ways(x, scatter, first, second):
    n_first = lax.axis_size(first)
    n_second = lax.axis_size(second)
    half = x.shape[1] // 2
    one = scatter(scatter(x[:, :half], first), second)
    other = (
        x[:, half:]
        .reshape(n_first, n_second, -1, half)
        .transpose(1, 0, 2, 3)
        .reshape(x.shape[0], half)
    )
    other = scatter(scatter(other, second), first)
    return jnp.concatenate([one, other], axis=1)


def bank_index():
    index = 0
    for name in BANK_AXES:
        index = index * lax.axis_size(name) + lax.axis_index(name)
    return index


def body(
    event_features,
    event_bins,
    positive,
    teacher_bank,
    in_weight,
    embedding_head_weight,
    membrane_decay_rate,
):
    per_device = positive.shape[0]
    bank_rows = teacher_bank.shape[0]
    onehot = (event_bins[:, None, :] == jnp.arange(TIME, dtype=jnp.int32)[None, :, None]).astype(
        jnp.bfloat16
    )
    binned = jnp.einsum(
        "ste,sec->stc", onehot, event_features, preferred_element_type=jnp.float32
    ).astype(jnp.bfloat16)
    flat_in = binned.reshape(per_device * TIME, C_IN)
    input_current = jnp.dot(flat_in, in_weight, preferred_element_type=jnp.float32).reshape(
        per_device, TIME, H
    )
    spike_train, leaky_neuron_backward = jax.vjp(
        partial(membrane_potential, membrane_decay_rate=membrane_decay_rate), input_current
    )
    spike_train_reduced = spike_train.astype(jnp.bfloat16)
    projected_embedding = jnp.dot(
        spike_train_reduced, embedding_head_weight, preferred_element_type=jnp.float32
    )
    length = jnp.sqrt(
        jnp.sum(projected_embedding * projected_embedding, axis=1, keepdims=True) + epsilon
    )
    query = projected_embedding / length
    query_low = query.astype(jnp.bfloat16)

    digits = jnp.stack([(positive >> 12) & 63, (positive >> 6) & 63, positive & 63], axis=1)
    code = jnp.zeros((per_device, CODE_COLS), jnp.bfloat16).at[:, :3].set(
        digits.astype(jnp.bfloat16)
    )
    gathered = jnp.concatenate([query_low, code], axis=1)
    for name in GATHER_ORDER:
        gathered = gather_relative(gathered, name)
    gathered_query = gathered[:, :D]
    gathered_digits = gathered[:, D : D + 3].astype(jnp.int32)
    gathered_pos = (
        gathered_digits[:, 0] * 4096 + gathered_digits[:, 1] * 64 + gathered_digits[:, 2]
    )

    start_row = bank_index() * bank_rows
    inverse = 1.0 / jnp.sqrt(
        jnp.sum(jnp.square(teacher_bank.astype(jnp.float32)), axis=1) + epsilon
    )
    local_index = gathered_pos - start_row
    is_owner = (local_index >= 0) & (local_index < bank_rows)
    local_index = jnp.clip(local_index, 0, bank_rows - 1)

    cosine_affinity_matrix = (
        jnp.dot(gathered_query, teacher_bank.T, preferred_element_type=jnp.float32)
        * inverse[None, :]
        / sharpening_divisor
    )
    exponent = jnp.exp(cosine_affinity_matrix)
    weights = (exponent * inverse[None, :]).astype(jnp.bfloat16)
    partition_part = jnp.sum(exponent, axis=1)
    column = lax.broadcasted_iota(jnp.int32, cosine_affinity_matrix.shape, 1)
    picked = jnp.sum(
        jnp.where(column == local_index[:, None], cosine_affinity_matrix, 0.0), axis=1
    )
    pos_part = jnp.where(is_owner, picked, 0.0)

    layout = list(reversed(GATHER_ORDER))
    stats = jnp.stack([partition_part, pos_part]).reshape(
        2, *[lax.axis_size(name) for name in layout], per_device
    )
    for name in layout:
        stats = sum_relative(stats, name, 1 + layout.index(name))
    stats = stats.reshape(2, -1)
    exponent_total = stats[0]
    matched_dot_value = stats[1]
    own_start = 0
    own_partition = lax.dynamic_slice_in_dim(exponent_total, own_start, per_device, 0)
    own_pos = lax.dynamic_slice_in_dim(matched_dot_value, own_start, per_device, 0)
    sample_loss = jnp.log(own_partition) - own_pos

    partial_sums = jnp.dot(weights, teacher_bank, preferred_element_type=jnp.float32)
    matched_entries = (
        jnp.take(teacher_bank, local_index, axis=0).astype(jnp.float32)
        * jnp.take(inverse, local_index)[:, None]
    )
    local_owned_rows = jnp.where(is_owner[:, None], matched_entries, 0.0)
    query_grad = (partial_sums / exponent_total[:, None] - local_owned_rows) / (
        sharpening_divisor * objective_divisor
    )
    query_grad = scatter_relative(query_grad, "bc")
    query_grad = scatter_two_ways(query_grad, scatter_relative, "bz", "bx")

    projection_gradient = (
        (query_grad - query * jnp.sum(query * query_grad, axis=1, keepdims=True)) / length
    ).astype(jnp.bfloat16)
    head_weight_piece = jnp.dot(
        spike_train_reduced.T, projection_gradient, preferred_element_type=jnp.float32
    )
    spike_train_gradient = jnp.dot(
        projection_gradient, embedding_head_weight.T, preferred_element_type=jnp.float32
    )
    (input_current_gradient,) = leaky_neuron_backward(spike_train_gradient)
    current_low = input_current_gradient.astype(jnp.bfloat16).reshape(per_device * TIME, H)
    in_part = jnp.dot(flat_in.T, current_low, preferred_element_type=jnp.float32)

    sizes = [lax.axis_size(name) for name in BANK_AXES]
    bank_size = sizes[0] * sizes[1] * sizes[2]
    in_share_rows = C_IN // bank_size
    head_share_rows = H // bank_size
    grads = jnp.concatenate(
        [
            in_part.reshape(bank_size, in_share_rows * H),
            head_weight_piece.reshape(bank_size, head_share_rows * D),
        ],
        axis=1,
    )
    order = [BANK_AXES.index(name) for name in reversed(GATHER_ORDER)]
    grads = (
        grads.reshape(*sizes, grads.shape[1])
        .transpose(*order, 3)
        .reshape(bank_size, grads.shape[1])
    )
    grads = scatter_absolute(grads, "bc")
    grads = scatter_two_ways(grads, scatter_absolute, "bz", "bx")
    grads = sum_all(grads, "dp")
    in_grad = grads[0, : in_share_rows * H].reshape(in_share_rows, H)
    head_weight_gradient = grads[0, in_share_rows * H :].reshape(head_share_rows, D)
    return (sample_loss, in_grad, head_weight_gradient)


def split_mesh(mesh):
    devices = mesh.devices
    column = devices[:, 0]
    try:
        xs = sorted({int(d.coords[0]) for d in column})
        zs = sorted({int(d.coords[2]) for d in column})
        cs = sorted({int(d.core_on_chip) for d in column})
        nx, nz, nc = len(xs), len(zs), len(cs)
        ok = nx * nz * nc == column.shape[0]
        for b, d in enumerate(column):
            want = (b // (nz * nc), (b // nc) % nz, b % nc)
            got = (xs.index(int(d.coords[0])), zs.index(int(d.coords[2])), cs.index(int(d.core_on_chip)))
            ok = ok and want == got
    except (AttributeError, IndexError, TypeError):
        ok = False
    if not ok:
        nx, nz, nc = 1, 1, column.shape[0]
    return Mesh(devices.reshape(nx, nz, nc, devices.shape[1]), SAMPLE_AXES)


def solution(mesh):
    split = split_mesh(mesh)
    in_specs = (
        P(SAMPLE_AXES, None, None),
        P(SAMPLE_AXES, None),
        P(SAMPLE_AXES),
        P(BANK_AXES, None),
        P(),
        P(),
        P(),
    )
    out_specs = (P(SAMPLE_AXES), P(BANK_AXES, None), P(BANK_AXES, None))
    return jax.shard_map(body, mesh=split, in_specs=in_specs, out_specs=out_specs, check_vma=False)
```

```python
from functools import partial

import jax
import jax.numpy as jnp
from jax import lax
from jax.sharding import Mesh
from jax.sharding import PartitionSpec as P

D = 1024
H = 512
C_IN = 128
TIME = 8


sharpening_divisor = 0.07
objective_divisor = 64.0
threshold = 1.0
sharpness = 4.0
epsilon = 1e-06

BANK_AXES = ("bx", "bz", "bc")
SAMPLE_AXES = ("bx", "bz", "bc", "dp")
GATHER_ORDER = ("bx", "bz", "bc")
CODE_COLS = 128


def membrane_potential(input_current, membrane_decay_rate):
    potential = jnp.zeros((input_current.shape[0], input_current.shape[2]), jnp.float32)
    spikes = jnp.zeros_like(potential)
    totals = jnp.zeros_like(potential)
    for moment in range(input_current.shape[1]):
        potential = membrane_decay_rate * potential + input_current[:, moment, :] - spikes
        spikes = jax.nn.sigmoid(sharpness * (potential - threshold))
        totals = totals + spikes
    return totals / input_current.shape[1]


def shift_pairs(name, shift):
    size = lax.axis_size(name)
    return [(j, (j + shift) % size) for j in range(size)]


def doubling(size):
    if size & (size - 1):
        return None
    steps = []
    step = 1
    while step < size:
        steps.append(step)
        step *= 2
    return steps


def gather_relative(x, name):
    size = lax.axis_size(name)
    steps = doubling(size)
    if steps is None:
        blocks = [x] + [lax.ppermute(x, name, shift_pairs(name, k)) for k in range(1, size)]
        return jnp.concatenate(blocks, axis=0)
    for step in steps:
        x = jnp.concatenate([x, lax.ppermute(x, name, shift_pairs(name, step))], axis=0)
    return x


def sum_relative(x, name, axis):
    size = lax.axis_size(name)
    steps = doubling(size)
    if steps is None:
        total = x
        for k in range(1, size):
            total = total + jnp.roll(lax.ppermute(x, name, shift_pairs(name, k)), k, axis=axis)
        return total
    for step in steps:
        x = x + jnp.roll(lax.ppermute(x, name, shift_pairs(name, step)), step, axis=axis)
    return x


def sum_all(x, name):
    size = lax.axis_size(name)
    steps = doubling(size)
    if steps is None:
        total = x
        for k in range(1, size):
            total = total + lax.ppermute(x, name, shift_pairs(name, k))
        return total
    for step in steps:
        x = x + lax.ppermute(x, name, shift_pairs(name, step))
    return x


def ring_scatter_sum(pick, name, size):
    total = pick(0)
    for k in range(1, size):
        total = total + lax.ppermute(pick(k), name, shift_pairs(name, -k))
    return total


def scatter_relative(x, name):
    size = lax.axis_size(name)
    blocks = x.reshape(size, x.shape[0] // size, *x.shape[1:])
    return ring_scatter_sum(lambda k: blocks[k], name, size)


def scatter_absolute(x, name):
    size = lax.axis_size(name)
    rows = x.shape[0] // size
    me = lax.axis_index(name)

    def pick(k):
        return lax.dynamic_slice_in_dim(x, ((me - k) % size) * rows, rows, 0)

    return ring_scatter_sum(pick, name, size)


def scatter_two_ways(x, scatter, first, second):
    n_first = lax.axis_size(first)
    n_second = lax.axis_size(second)
    half = x.shape[1] // 2
    one = scatter(scatter(x[:, :half], first), second)
    other = (
        x[:, half:]
        .reshape(n_first, n_second, -1, half)
        .transpose(1, 0, 2, 3)
        .reshape(x.shape[0], half)
    )
    other = scatter(scatter(other, second), first)
    return jnp.concatenate([one, other], axis=1)


def bank_index():
    index = 0
    for name in BANK_AXES:
        index = index * lax.axis_size(name) + lax.axis_index(name)
    return index


def body(
    event_features,
    event_bins,
    positive,
    teacher_bank,
    in_weight,
    embedding_head_weight,
    membrane_decay_rate,
):
    per_device = positive.shape[0]
    bank_rows = teacher_bank.shape[0]
    onehot = (event_bins[:, None, :] == jnp.arange(TIME, dtype=jnp.int32)[None, :, None]).astype(
        jnp.bfloat16
    )
    binned = jnp.einsum(
        "ste,sec->stc", onehot, event_features, preferred_element_type=jnp.float32
    ).astype(jnp.bfloat16)
    flat_in = binned.reshape(per_device * TIME, C_IN)
    input_current = jnp.dot(flat_in, in_weight, preferred_element_type=jnp.float32).reshape(
        per_device, TIME, H
    )
    spike_train, leaky_neuron_backward = jax.vjp(
        partial(membrane_potential, membrane_decay_rate=membrane_decay_rate), input_current
    )
    spike_train_reduced = spike_train.astype(jnp.bfloat16)
    projected_embedding = jnp.dot(
        spike_train_reduced, embedding_head_weight, preferred_element_type=jnp.float32
    )
    length = jnp.sqrt(
        jnp.sum(projected_embedding * projected_embedding, axis=1, keepdims=True) + epsilon
    )
    query = projected_embedding / length
    query_low = query.astype(jnp.bfloat16)

    digits = jnp.stack([(positive >> 12) & 63, (positive >> 6) & 63, positive & 63], axis=1)
    code = jnp.zeros((per_device, CODE_COLS), jnp.bfloat16).at[:, :3].set(
        digits.astype(jnp.bfloat16)
    )
    gathered = jnp.concatenate([query_low, code], axis=1)
    for name in GATHER_ORDER:
        gathered = gather_relative(gathered, name)
    gathered_query = gathered[:, :D]
    gathered_digits = gathered[:, D : D + 3].astype(jnp.int32)
    gathered_pos = (
        gathered_digits[:, 0] * 4096 + gathered_digits[:, 1] * 64 + gathered_digits[:, 2]
    )

    start_row = bank_index() * bank_rows
    inverse = 1.0 / jnp.sqrt(
        jnp.sum(jnp.square(teacher_bank.astype(jnp.float32)), axis=1) + epsilon
    )
    local_index = gathered_pos - start_row
    is_owner = (local_index >= 0) & (local_index < bank_rows)
    local_index = jnp.clip(local_index, 0, bank_rows - 1)

    cosine_affinity_matrix = (
        jnp.dot(gathered_query, teacher_bank.T, preferred_element_type=jnp.float32)
        * inverse[None, :]
        / sharpening_divisor
    )
    exponent = jnp.exp(cosine_affinity_matrix)
    weights = (exponent * inverse[None, :]).astype(jnp.bfloat16)
    partition_part = jnp.sum(exponent, axis=1)
    column = lax.broadcasted_iota(jnp.int32, cosine_affinity_matrix.shape, 1)
    picked = jnp.sum(
        jnp.where(column == local_index[:, None], cosine_affinity_matrix, 0.0), axis=1
    )
    pos_part = jnp.where(is_owner, picked, 0.0)

    layout = list(reversed(GATHER_ORDER))
    stats = jnp.stack([partition_part, pos_part]).reshape(
        2, *[lax.axis_size(name) for name in layout], per_device
    )
    for name in layout:
        stats = sum_relative(stats, name, 1 + layout.index(name))
    stats = stats.reshape(2, -1)
    exponent_total = stats[0]
    matched_dot_value = stats[1]
    own_start = 0
    own_partition = lax.dynamic_slice_in_dim(exponent_total, own_start, per_device, 0)
    own_pos = lax.dynamic_slice_in_dim(matched_dot_value, own_start, per_device, 0)
    sample_loss = jnp.log(own_partition) - own_pos

    partial_sums = jnp.dot(weights, teacher_bank, preferred_element_type=jnp.float32)
    matched_entries = (
        jnp.take(teacher_bank, local_index, axis=0).astype(jnp.float32)
        * jnp.take(inverse, local_index)[:, None]
    )
    local_owned_rows = jnp.where(is_owner[:, None], matched_entries, 0.0)
    query_grad = (partial_sums / exponent_total[:, None] - local_owned_rows) / (
        sharpening_divisor * objective_divisor
    )
    query_grad = scatter_relative(query_grad, "bc")
    query_grad = scatter_two_ways(query_grad, scatter_relative, "bz", "bx")

    projection_gradient = (
        (query_grad - query * jnp.sum(query * query_grad, axis=1, keepdims=True)) / length
    ).astype(jnp.bfloat16)
    head_weight_piece = jnp.dot(
        spike_train_reduced.T, projection_gradient, preferred_element_type=jnp.float32
    )
    spike_train_gradient = jnp.dot(
        projection_gradient, embedding_head_weight.T, preferred_element_type=jnp.float32
    )
    (input_current_gradient,) = leaky_neuron_backward(spike_train_gradient)
    current_low = input_current_gradient.astype(jnp.bfloat16).reshape(per_device * TIME, H)
    in_part = jnp.dot(flat_in.T, current_low, preferred_element_type=jnp.float32)

    sizes = [lax.axis_size(name) for name in BANK_AXES]
    bank_size = sizes[0] * sizes[1] * sizes[2]
    in_share_rows = C_IN // bank_size
    head_share_rows = H // bank_size
    grads = jnp.concatenate(
        [
            in_part.reshape(bank_size, in_share_rows * H),
            head_weight_piece.reshape(bank_size, head_share_rows * D),
        ],
        axis=1,
    )
    order = [BANK_AXES.index(name) for name in reversed(GATHER_ORDER)]
    grads = (
        grads.reshape(*sizes, grads.shape[1])
        .transpose(*order, 3)
        .reshape(bank_size, grads.shape[1])
    )
    grads = scatter_absolute(grads, "bc")
    grads = scatter_two_ways(grads, scatter_absolute, "bz", "bx")
    grads = sum_all(grads, "dp")
    in_grad = grads[0, : in_share_rows * H].reshape(in_share_rows, H)
    head_weight_gradient = grads[0, in_share_rows * H :].reshape(head_share_rows, D)
    return (sample_loss, in_grad, head_weight_gradient)


def split_mesh(mesh):
    devices = mesh.devices
    column = devices[:, 0]
    try:
        xs = sorted({int(d.coords[0]) for d in column})
        zs = sorted({int(d.coords[2]) for d in column})
        cs = sorted({int(d.core_on_chip) for d in column})
        nx, nz, nc = len(xs), len(zs), len(cs)
        ok = nx * nz * nc == column.shape[0]
        for b, d in enumerate(column):
            want = (b // (nz * nc), (b // nc) % nz, b % nc)
            got = (xs.index(int(d.coords[0])), zs.index(int(d.coords[2])), cs.index(int(d.core_on_chip)))
            ok = ok and want == got
    except (AttributeError, IndexError, TypeError):
        ok = False
    if not ok:
        nx, nz, nc = 1, 1, column.shape[0]
    return Mesh(devices.reshape(nx, nz, nc, devices.shape[1]), SAMPLE_AXES)


def solution(mesh):
    split = split_mesh(mesh)
    in_specs = (
        P(SAMPLE_AXES, None, None),
        P(SAMPLE_AXES, None),
        P(SAMPLE_AXES),
        P(BANK_AXES, None),
        P(),
        P(),
        P(),
    )
    out_specs = (P(SAMPLE_AXES), P(BANK_AXES, None), P(BANK_AXES, None))
    return jax.shard_map(body, mesh=split, in_specs=in_specs, out_specs=out_specs, check_vma=False)
```

```python
from functools import partial

import jax
import jax.numpy as jnp
from jax import lax
from jax.sharding import Mesh
from jax.sharding import PartitionSpec as P

D = 1024
H = 512
C_IN = 128
TIME = 8


sharpening_divisor = 0.07
objective_divisor = 64.0
threshold = 1.0
sharpness = 4.0
epsilon = 1e-06

BANK_AXES = ("bx", "bz", "bc")
SAMPLE_AXES = ("bx", "bz", "bc", "dp")
GATHER_ORDER = ("bx", "bz", "bc")
CODE_COLS = 128


def membrane_potential(input_current, membrane_decay_rate):
    potential = jnp.zeros((input_current.shape[0], input_current.shape[2]), jnp.float32)
    spikes = jnp.zeros_like(potential)
    totals = jnp.zeros_like(potential)
    for moment in range(input_current.shape[1]):
        potential = membrane_decay_rate * potential + input_current[:, moment, :] - spikes
        spikes = jax.nn.sigmoid(sharpness * (potential - threshold))
        totals = totals + spikes
    return totals / input_current.shape[1]


def shift_pairs(name, shift):
    size = lax.axis_size(name)
    return [(j, (j + shift) % size) for j in range(size)]


def gather_relative(x, name):
    size = lax.axis_size(name)
    blocks = [x] + [lax.ppermute(x, name, shift_pairs(name, k)) for k in range(1, size)]
    return jnp.concatenate(blocks, axis=0)


def sum_relative(x, name, axis):
    size = lax.axis_size(name)
    total = x
    for k in range(1, size):
        total = total + jnp.roll(lax.ppermute(x, name, shift_pairs(name, k)), k, axis=axis)
    return total


def joint_shifts(names):
    sizes = [lax.axis_size(name) for name in names]
    return [(a, c) for a in range(sizes[0]) for c in range(sizes[1])]


def joint_pairs(names, shift):
    sizes = [lax.axis_size(name) for name in names]
    pairs = []
    for a in range(sizes[0]):
        for c in range(sizes[1]):
            target = ((a + shift[0]) % sizes[0]) * sizes[1] + (c + shift[1]) % sizes[1]
            pairs.append((a * sizes[1] + c, target))
    return pairs


def gather_joint(x, names):
    blocks = [
        x if shift == (0, 0) else lax.ppermute(x, names, joint_pairs(names, shift))
        for shift in joint_shifts(names)
    ]
    return jnp.concatenate(blocks, axis=0)


def sum_joint_relative(x, names, axes):
    total = x
    for shift in joint_shifts(names)[1:]:
        total = total + jnp.roll(lax.ppermute(x, names, joint_pairs(names, shift)), shift, axis=axes)
    return total


def sum_all(x, name):
    size = lax.axis_size(name)
    total = x
    for k in range(1, size):
        total = total + lax.ppermute(x, name, shift_pairs(name, k))
    return total


def ring_scatter_sum(pick, name, size):
    total = pick(0)
    for k in range(1, size):
        total = total + lax.ppermute(pick(k), name, shift_pairs(name, -k))
    return total


def scatter_relative(x, name):
    size = lax.axis_size(name)
    blocks = x.reshape(size, x.shape[0] // size, *x.shape[1:])
    return ring_scatter_sum(lambda k: blocks[k], name, size)


def scatter_absolute(x, name):
    size = lax.axis_size(name)
    rows = x.shape[0] // size
    me = lax.axis_index(name)

    def pick(k):
        return lax.dynamic_slice_in_dim(x, ((me - k) % size) * rows, rows, 0)

    return ring_scatter_sum(pick, name, size)


def scatter_two_ways(x, scatter, first, second):
    n_first = lax.axis_size(first)
    n_second = lax.axis_size(second)
    half = x.shape[1] // 2
    one = scatter(scatter(x[:, :half], first), second)
    other = (
        x[:, half:]
        .reshape(n_first, n_second, -1, half)
        .transpose(1, 0, 2, 3)
        .reshape(x.shape[0], half)
    )
    other = scatter(scatter(other, second), first)
    return jnp.concatenate([one, other], axis=1)


def bank_index():
    index = 0
    for name in BANK_AXES:
        index = index * lax.axis_size(name) + lax.axis_index(name)
    return index


def body(
    event_features,
    event_bins,
    positive,
    teacher_bank,
    in_weight,
    embedding_head_weight,
    membrane_decay_rate,
):
    per_device = positive.shape[0]
    bank_rows = teacher_bank.shape[0]
    onehot = (event_bins[:, None, :] == jnp.arange(TIME, dtype=jnp.int32)[None, :, None]).astype(
        jnp.bfloat16
    )
    binned = jnp.einsum(
        "ste,sec->stc", onehot, event_features, preferred_element_type=jnp.float32
    ).astype(jnp.bfloat16)
    flat_in = binned.reshape(per_device * TIME, C_IN)
    input_current = jnp.dot(flat_in, in_weight, preferred_element_type=jnp.float32).reshape(
        per_device, TIME, H
    )
    spike_train, leaky_neuron_backward = jax.vjp(
        partial(membrane_potential, membrane_decay_rate=membrane_decay_rate), input_current
    )
    spike_train_reduced = spike_train.astype(jnp.bfloat16)
    projected_embedding = jnp.dot(
        spike_train_reduced, embedding_head_weight, preferred_element_type=jnp.float32
    )
    length = jnp.sqrt(
        jnp.sum(projected_embedding * projected_embedding, axis=1, keepdims=True) + epsilon
    )
    query = projected_embedding / length
    query_low = query.astype(jnp.bfloat16)

    digits = jnp.stack([(positive >> 12) & 63, (positive >> 6) & 63, positive & 63], axis=1)
    code = jnp.zeros((per_device, CODE_COLS), jnp.bfloat16).at[:, :3].set(
        digits.astype(jnp.bfloat16)
    )
    gathered = jnp.concatenate([query_low, code], axis=1)
    gathered = gather_joint(gathered, ("bx", "bc"))
    gathered = gather_relative(gathered, "bz")
    gathered_query = gathered[:, :D]
    gathered_digits = gathered[:, D : D + 3].astype(jnp.int32)
    gathered_pos = (
        gathered_digits[:, 0] * 4096 + gathered_digits[:, 1] * 64 + gathered_digits[:, 2]
    )

    start_row = bank_index() * bank_rows
    inverse = 1.0 / jnp.sqrt(
        jnp.sum(jnp.square(teacher_bank.astype(jnp.float32)), axis=1) + epsilon
    )
    local_index = gathered_pos - start_row
    is_owner = (local_index >= 0) & (local_index < bank_rows)
    local_index = jnp.clip(local_index, 0, bank_rows - 1)

    cosine_affinity_matrix = (
        jnp.dot(gathered_query, teacher_bank.T, preferred_element_type=jnp.float32)
        * inverse[None, :]
        / sharpening_divisor
    )
    exponent = jnp.exp(cosine_affinity_matrix)
    weights = (exponent * inverse[None, :]).astype(jnp.bfloat16)
    partition_part = jnp.sum(exponent, axis=1)
    column = lax.broadcasted_iota(jnp.int32, cosine_affinity_matrix.shape, 1)
    picked = jnp.sum(
        jnp.where(column == local_index[:, None], cosine_affinity_matrix, 0.0), axis=1
    )
    pos_part = jnp.where(is_owner, picked, 0.0)

    n_x, n_z, n_c = [lax.axis_size(name) for name in BANK_AXES]
    stats = jnp.stack([partition_part, pos_part]).reshape(2, n_z, n_x, n_c, per_device)
    stats = sum_relative(stats, "bz", 1)
    stats = sum_joint_relative(stats, ("bx", "bc"), (2, 3))
    stats = stats.reshape(2, -1)
    exponent_total = stats[0]
    matched_dot_value = stats[1]
    own_start = 0
    own_partition = lax.dynamic_slice_in_dim(exponent_total, own_start, per_device, 0)
    own_pos = lax.dynamic_slice_in_dim(matched_dot_value, own_start, per_device, 0)
    sample_loss = jnp.log(own_partition) - own_pos

    partial_sums = jnp.dot(weights, teacher_bank, preferred_element_type=jnp.float32)
    matched_entries = (
        jnp.take(teacher_bank, local_index, axis=0).astype(jnp.float32)
        * jnp.take(inverse, local_index)[:, None]
    )
    local_owned_rows = jnp.where(is_owner[:, None], matched_entries, 0.0)
    query_grad = (partial_sums / exponent_total[:, None] - local_owned_rows) / (
        sharpening_divisor * objective_divisor
    )
    query_grad = (
        query_grad.reshape(n_z, n_x, n_c, per_device, D).transpose(2, 0, 1, 3, 4).reshape(-1, D)
    )
    query_grad = scatter_relative(query_grad, "bc")
    query_grad = scatter_two_ways(query_grad, scatter_relative, "bz", "bx")

    projection_gradient = (
        (query_grad - query * jnp.sum(query * query_grad, axis=1, keepdims=True)) / length
    ).astype(jnp.bfloat16)
    head_weight_piece = jnp.dot(
        spike_train_reduced.T, projection_gradient, preferred_element_type=jnp.float32
    )
    spike_train_gradient = jnp.dot(
        projection_gradient, embedding_head_weight.T, preferred_element_type=jnp.float32
    )
    (input_current_gradient,) = leaky_neuron_backward(spike_train_gradient)
    current_low = input_current_gradient.astype(jnp.bfloat16).reshape(per_device * TIME, H)
    in_part = jnp.dot(flat_in.T, current_low, preferred_element_type=jnp.float32)

    sizes = [lax.axis_size(name) for name in BANK_AXES]
    bank_size = sizes[0] * sizes[1] * sizes[2]
    in_share_rows = C_IN // bank_size
    head_share_rows = H // bank_size
    grads = jnp.concatenate(
        [
            in_part.reshape(bank_size, in_share_rows * H),
            head_weight_piece.reshape(bank_size, head_share_rows * D),
        ],
        axis=1,
    )
    order = [BANK_AXES.index(name) for name in reversed(GATHER_ORDER)]
    grads = (
        grads.reshape(*sizes, grads.shape[1])
        .transpose(*order, 3)
        .reshape(bank_size, grads.shape[1])
    )
    grads = scatter_absolute(grads, "bc")
    grads = scatter_two_ways(grads, scatter_absolute, "bz", "bx")
    grads = sum_all(grads, "dp")
    in_grad = grads[0, : in_share_rows * H].reshape(in_share_rows, H)
    head_weight_gradient = grads[0, in_share_rows * H :].reshape(head_share_rows, D)
    return (sample_loss, in_grad, head_weight_gradient)


def split_mesh(mesh):
    devices = mesh.devices
    column = devices[:, 0]
    try:
        xs = sorted({int(d.coords[0]) for d in column})
        zs = sorted({int(d.coords[2]) for d in column})
        cs = sorted({int(d.core_on_chip) for d in column})
        nx, nz, nc = len(xs), len(zs), len(cs)
        ok = nx * nz * nc == column.shape[0]
        for b, d in enumerate(column):
            want = (b // (nz * nc), (b // nc) % nz, b % nc)
            got = (xs.index(int(d.coords[0])), zs.index(int(d.coords[2])), cs.index(int(d.core_on_chip)))
            ok = ok and want == got
    except (AttributeError, IndexError, TypeError):
        ok = False
    if not ok:
        nx, nz, nc = 1, 1, column.shape[0]
    return Mesh(devices.reshape(nx, nz, nc, devices.shape[1]), SAMPLE_AXES)


def solution(mesh):
    split = split_mesh(mesh)
    in_specs = (
        P(SAMPLE_AXES, None, None),
        P(SAMPLE_AXES, None),
        P(SAMPLE_AXES),
        P(BANK_AXES, None),
        P(),
        P(),
        P(),
    )
    out_specs = (P(SAMPLE_AXES), P(BANK_AXES, None), P(BANK_AXES, None))
    return jax.shard_map(body, mesh=split, in_specs=in_specs, out_specs=out_specs, check_vma=False)
```

```python
from functools import partial

import jax
import jax.numpy as jnp
from jax import lax
from jax.sharding import Mesh
from jax.sharding import PartitionSpec as P

D = 1024
H = 512
C_IN = 128
TIME = 8


sharpening_divisor = 0.07
objective_divisor = 64.0
threshold = 1.0
sharpness = 4.0
epsilon = 1e-06

BANK_AXES = ("bx", "bz", "bc")
SAMPLE_AXES = ("bx", "bz", "bc", "dp")
GATHER_ORDER = ("bx", "bz", "bc")
CODE_COLS = 128


def membrane_potential(input_current, membrane_decay_rate):
    potential = jnp.zeros((input_current.shape[0], input_current.shape[2]), jnp.float32)
    spikes = jnp.zeros_like(potential)
    totals = jnp.zeros_like(potential)
    for moment in range(input_current.shape[1]):
        potential = membrane_decay_rate * potential + input_current[:, moment, :] - spikes
        spikes = jax.nn.sigmoid(sharpness * (potential - threshold))
        totals = totals + spikes
    return totals / input_current.shape[1]


def shift_pairs(name, shift):
    size = lax.axis_size(name)
    return [(j, (j + shift) % size) for j in range(size)]


def gather_relative(x, name):
    size = lax.axis_size(name)
    blocks = [x] + [lax.ppermute(x, name, shift_pairs(name, k)) for k in range(1, size)]
    return jnp.concatenate(blocks, axis=0)


def sum_relative(x, name, axis):
    size = lax.axis_size(name)
    total = x
    for k in range(1, size):
        total = total + jnp.roll(lax.ppermute(x, name, shift_pairs(name, k)), k, axis=axis)
    return total


def sum_all(x, name):
    size = lax.axis_size(name)
    total = x
    for k in range(1, size):
        total = total + lax.ppermute(x, name, shift_pairs(name, k))
    return total


def ring_scatter_sum(pick, name, size):
    total = pick(0)
    for k in range(1, size):
        total = total + lax.ppermute(pick(k), name, shift_pairs(name, -k))
    return total


def scatter_relative(x, name):
    size = lax.axis_size(name)
    blocks = x.reshape(size, x.shape[0] // size, *x.shape[1:])
    return ring_scatter_sum(lambda k: blocks[k], name, size)


def scatter_absolute(x, name):
    size = lax.axis_size(name)
    rows = x.shape[0] // size
    me = lax.axis_index(name)

    def pick(k):
        return lax.dynamic_slice_in_dim(x, ((me - k) % size) * rows, rows, 0)

    return ring_scatter_sum(pick, name, size)


def scatter_two_ways(x, scatter, first, second):
    n_first = lax.axis_size(first)
    n_second = lax.axis_size(second)
    half = x.shape[1] // 2
    one = scatter(scatter(x[:, :half], first), second)
    other = (
        x[:, half:]
        .reshape(n_first, n_second, -1, half)
        .transpose(1, 0, 2, 3)
        .reshape(x.shape[0], half)
    )
    other = scatter(scatter(other, second), first)
    return jnp.concatenate([one, other], axis=1)


def bank_index():
    index = 0
    for name in BANK_AXES:
        index = index * lax.axis_size(name) + lax.axis_index(name)
    return index


def body(
    event_features,
    event_bins,
    positive,
    teacher_bank,
    in_weight,
    embedding_head_weight,
    membrane_decay_rate,
):
    per_device = positive.shape[0]
    bank_rows = teacher_bank.shape[0]
    onehot = (event_bins[:, None, :] == jnp.arange(TIME, dtype=jnp.int32)[None, :, None]).astype(
        jnp.bfloat16
    )
    binned = jnp.einsum(
        "ste,sec->stc", onehot, event_features, preferred_element_type=jnp.float32
    ).astype(jnp.bfloat16)
    flat_in = binned.reshape(per_device * TIME, C_IN)
    input_current = jnp.dot(flat_in, in_weight, preferred_element_type=jnp.float32).reshape(
        per_device, TIME, H
    )
    spike_train, leaky_neuron_backward = jax.vjp(
        partial(membrane_potential, membrane_decay_rate=membrane_decay_rate), input_current
    )
    spike_train_reduced = spike_train.astype(jnp.bfloat16)
    projected_embedding = jnp.dot(
        spike_train_reduced, embedding_head_weight, preferred_element_type=jnp.float32
    )
    length = jnp.sqrt(
        jnp.sum(projected_embedding * projected_embedding, axis=1, keepdims=True) + epsilon
    )
    query = projected_embedding / length
    query_low = query.astype(jnp.bfloat16)

    digits = jnp.stack([(positive >> 12) & 63, (positive >> 6) & 63, positive & 63], axis=1)
    code = jnp.zeros((per_device, CODE_COLS), jnp.bfloat16).at[:, :3].set(
        digits.astype(jnp.bfloat16)
    )
    gathered = jnp.concatenate([query_low, code], axis=1)
    for name in GATHER_ORDER:
        gathered = gather_relative(gathered, name)
    gathered_query = gathered[:, :D]
    gathered_digits = gathered[:, D : D + 3].astype(jnp.int32)
    gathered_pos = (
        gathered_digits[:, 0] * 4096 + gathered_digits[:, 1] * 64 + gathered_digits[:, 2]
    )

    start_row = bank_index() * bank_rows
    inverse = 1.0 / jnp.sqrt(
        jnp.sum(jnp.square(teacher_bank.astype(jnp.float32)), axis=1) + epsilon
    )
    local_index = gathered_pos - start_row
    is_owner = (local_index >= 0) & (local_index < bank_rows)
    local_index = jnp.clip(local_index, 0, bank_rows - 1)

    cosine_affinity_matrix = (
        jnp.dot(gathered_query, teacher_bank.T, preferred_element_type=jnp.float32)
        * inverse[None, :]
        / sharpening_divisor
    )
    exponent = jnp.exp(cosine_affinity_matrix)
    weights = (exponent * inverse[None, :]).astype(jnp.bfloat16)
    partition_part = jnp.sum(exponent, axis=1)
    column = lax.broadcasted_iota(jnp.int32, cosine_affinity_matrix.shape, 1)
    picked = jnp.sum(
        jnp.where(column == local_index[:, None], cosine_affinity_matrix, 0.0), axis=1
    )
    pos_part = jnp.where(is_owner, picked, 0.0)

    layout = list(reversed(GATHER_ORDER))
    stats = jnp.stack([partition_part, pos_part]).reshape(
        2, *[lax.axis_size(name) for name in layout], per_device
    )
    for name in layout:
        stats = sum_relative(stats, name, 1 + layout.index(name))
    stats = stats.reshape(2, -1)
    exponent_total = stats[0]
    matched_dot_value = stats[1]
    own_start = 0
    own_partition = lax.dynamic_slice_in_dim(exponent_total, own_start, per_device, 0)
    own_pos = lax.dynamic_slice_in_dim(matched_dot_value, own_start, per_device, 0)
    sample_loss = jnp.log(own_partition) - own_pos

    partial_sums = jnp.dot(weights, teacher_bank, preferred_element_type=jnp.float32)
    owned = (column == local_index[:, None]) & is_owner[:, None]
    owned_rows = jnp.dot(
        owned.astype(jnp.bfloat16), teacher_bank, preferred_element_type=jnp.float32
    )
    owned_inverse = jnp.sum(jnp.where(owned, inverse[None, :], 0.0), axis=1)
    local_owned_rows = owned_rows * owned_inverse[:, None]
    query_grad = (partial_sums / exponent_total[:, None] - local_owned_rows) / (
        sharpening_divisor * objective_divisor
    )
    query_grad = scatter_relative(query_grad, "bc")
    query_grad = scatter_two_ways(query_grad, scatter_relative, "bz", "bx")

    projection_gradient = (
        (query_grad - query * jnp.sum(query * query_grad, axis=1, keepdims=True)) / length
    ).astype(jnp.bfloat16)
    head_weight_piece = jnp.dot(
        spike_train_reduced.T, projection_gradient, preferred_element_type=jnp.float32
    )
    spike_train_gradient = jnp.dot(
        projection_gradient, embedding_head_weight.T, preferred_element_type=jnp.float32
    )
    (input_current_gradient,) = leaky_neuron_backward(spike_train_gradient)
    current_low = input_current_gradient.astype(jnp.bfloat16).reshape(per_device * TIME, H)
    in_part = jnp.dot(flat_in.T, current_low, preferred_element_type=jnp.float32)

    sizes = [lax.axis_size(name) for name in BANK_AXES]
    bank_size = sizes[0] * sizes[1] * sizes[2]
    in_share_rows = C_IN // bank_size
    head_share_rows = H // bank_size
    grads = jnp.concatenate(
        [
            in_part.reshape(bank_size, in_share_rows * H),
            head_weight_piece.reshape(bank_size, head_share_rows * D),
        ],
        axis=1,
    )
    order = [BANK_AXES.index(name) for name in reversed(GATHER_ORDER)]
    grads = (
        grads.reshape(*sizes, grads.shape[1])
        .transpose(*order, 3)
        .reshape(bank_size, grads.shape[1])
    )
    grads = scatter_absolute(grads, "bc")
    grads = scatter_two_ways(grads, scatter_absolute, "bz", "bx")
    grads = sum_all(grads, "dp")
    in_grad = grads[0, : in_share_rows * H].reshape(in_share_rows, H)
    head_weight_gradient = grads[0, in_share_rows * H :].reshape(head_share_rows, D)
    return (sample_loss, in_grad, head_weight_gradient)


def split_mesh(mesh):
    devices = mesh.devices
    column = devices[:, 0]
    try:
        xs = sorted({int(d.coords[0]) for d in column})
        zs = sorted({int(d.coords[2]) for d in column})
        cs = sorted({int(d.core_on_chip) for d in column})
        nx, nz, nc = len(xs), len(zs), len(cs)
        ok = nx * nz * nc == column.shape[0]
        for b, d in enumerate(column):
            want = (b // (nz * nc), (b // nc) % nz, b % nc)
            got = (xs.index(int(d.coords[0])), zs.index(int(d.coords[2])), cs.index(int(d.core_on_chip)))
            ok = ok and want == got
    except (AttributeError, IndexError, TypeError):
        ok = False
    if not ok:
        nx, nz, nc = 1, 1, column.shape[0]
    return Mesh(devices.reshape(nx, nz, nc, devices.shape[1]), SAMPLE_AXES)


def solution(mesh):
    split = split_mesh(mesh)
    in_specs = (
        P(SAMPLE_AXES, None, None),
        P(SAMPLE_AXES, None),
        P(SAMPLE_AXES),
        P(BANK_AXES, None),
        P(),
        P(),
        P(),
    )
    out_specs = (P(SAMPLE_AXES), P(BANK_AXES, None), P(BANK_AXES, None))
    return jax.shard_map(body, mesh=split, in_specs=in_specs, out_specs=out_specs, check_vma=False)
```

```python
from functools import partial

import jax
import numpy as np
import jax.numpy as jnp
from jax import lax
from jax.sharding import Mesh
from jax.sharding import PartitionSpec as P

D = 1024
H = 512
C_IN = 128
TIME = 8


sharpening_divisor = 0.07
objective_divisor = 64.0
threshold = 1.0
sharpness = 4.0
epsilon = 1e-06

BANK_AXES = ("bx", "bz", "bc")
SAMPLE_AXES = ("bx", "bz", "bc", "dp")
GATHER_ORDER = ("bx", "bz", "bc")
CODE_COLS = 128


def membrane_potential(input_current, membrane_decay_rate):
    potential = jnp.zeros((input_current.shape[0], input_current.shape[2]), jnp.float32)
    spikes = jnp.zeros_like(potential)
    totals = jnp.zeros_like(potential)
    for moment in range(input_current.shape[1]):
        potential = membrane_decay_rate * potential + input_current[:, moment, :] - spikes
        spikes = jax.nn.sigmoid(sharpness * (potential - threshold))
        totals = totals + spikes
    return totals / input_current.shape[1]


def shift_pairs(name, shift):
    size = lax.axis_size(name)
    return [(j, (j + shift) % size) for j in range(size)]


def gather_relative(x, name):
    size = lax.axis_size(name)
    blocks = [x] + [lax.ppermute(x, name, shift_pairs(name, k)) for k in range(1, size)]
    return jnp.concatenate(blocks, axis=0)


def sum_relative(x, name, axis):
    size = lax.axis_size(name)
    total = x
    for k in range(1, size):
        total = total + jnp.roll(lax.ppermute(x, name, shift_pairs(name, k)), k, axis=axis)
    return total


def sum_all(x, name):
    size = lax.axis_size(name)
    total = x
    for k in range(1, size):
        total = total + lax.ppermute(x, name, shift_pairs(name, k))
    return total


def ring_scatter_sum(pick, name, size):
    total = pick(0)
    for k in range(1, size):
        total = total + lax.ppermute(pick(k), name, shift_pairs(name, -k))
    return total


def scatter_relative(x, name):
    size = lax.axis_size(name)
    blocks = x.reshape(size, x.shape[0] // size, *x.shape[1:])
    return ring_scatter_sum(lambda k: blocks[k], name, size)


def scatter_absolute(x, name):
    size = lax.axis_size(name)
    rows = x.shape[0] // size
    me = lax.axis_index(name)

    def pick(k):
        return lax.dynamic_slice_in_dim(x, ((me - k) % size) * rows, rows, 0)

    return ring_scatter_sum(pick, name, size)


def scatter_two_ways(x, scatter, first, second):
    n_first = lax.axis_size(first)
    n_second = lax.axis_size(second)
    half = x.shape[1] // 2
    one = scatter(scatter(x[:, :half], first), second)
    other = (
        x[:, half:]
        .reshape(n_first, n_second, -1, half)
        .transpose(1, 0, 2, 3)
        .reshape(x.shape[0], half)
    )
    other = scatter(scatter(other, second), first)
    return jnp.concatenate([one, other], axis=1)


def bank_index():
    index = 0
    for name in BANK_AXES:
        index = index * lax.axis_size(name) + lax.axis_index(name)
    return index


def body(
    event_features,
    event_bins,
    positive,
    teacher_bank,
    in_weight,
    embedding_head_weight,
    membrane_decay_rate,
):
    per_device = positive.shape[0]
    bank_rows = teacher_bank.shape[0]
    onehot = (event_bins[:, None, :] == jnp.arange(TIME, dtype=jnp.int32)[None, :, None]).astype(
        jnp.bfloat16
    )
    binned = jnp.einsum(
        "ste,sec->stc", onehot, event_features, preferred_element_type=jnp.float32
    ).astype(jnp.bfloat16)
    flat_in = binned.reshape(per_device * TIME, C_IN)
    input_current = jnp.dot(flat_in, in_weight, preferred_element_type=jnp.float32).reshape(
        per_device, TIME, H
    )
    spike_train, leaky_neuron_backward = jax.vjp(
        partial(membrane_potential, membrane_decay_rate=membrane_decay_rate), input_current
    )
    spike_train_reduced = spike_train.astype(jnp.bfloat16)
    projected_embedding = jnp.dot(
        spike_train_reduced, embedding_head_weight, preferred_element_type=jnp.float32
    )
    length = jnp.sqrt(
        jnp.sum(projected_embedding * projected_embedding, axis=1, keepdims=True) + epsilon
    )
    query = projected_embedding / length
    query_low = query.astype(jnp.bfloat16)

    digits = jnp.stack([(positive >> 12) & 63, (positive >> 6) & 63, positive & 63], axis=1)
    code = jnp.zeros((per_device, CODE_COLS), jnp.bfloat16).at[:, :3].set(
        digits.astype(jnp.bfloat16)
    )
    gathered = jnp.concatenate([query_low, code], axis=1)
    for name in GATHER_ORDER:
        gathered = gather_relative(gathered, name)
    gathered_query = gathered[:, :D]
    gathered_digits = gathered[:, D : D + 3].astype(jnp.int32)
    gathered_pos = (
        gathered_digits[:, 0] * 4096 + gathered_digits[:, 1] * 64 + gathered_digits[:, 2]
    )

    start_row = bank_index() * bank_rows
    inverse = 1.0 / jnp.sqrt(
        jnp.sum(jnp.square(teacher_bank.astype(jnp.float32)), axis=1) + epsilon
    )
    local_index = gathered_pos - start_row
    is_owner = (local_index >= 0) & (local_index < bank_rows)
    local_index = jnp.clip(local_index, 0, bank_rows - 1)

    cosine_affinity_matrix = (
        jnp.dot(gathered_query, teacher_bank.T, preferred_element_type=jnp.float32)
        * inverse[None, :]
        / sharpening_divisor
    )
    exponent = jnp.exp(cosine_affinity_matrix)
    weights = (exponent * inverse[None, :]).astype(jnp.bfloat16)
    partition_part = jnp.sum(exponent, axis=1)
    column = lax.broadcasted_iota(jnp.int32, cosine_affinity_matrix.shape, 1)
    picked = jnp.sum(
        jnp.where(column == local_index[:, None], cosine_affinity_matrix, 0.0), axis=1
    )
    pos_part = jnp.where(is_owner, picked, 0.0)

    layout = list(reversed(GATHER_ORDER))
    stats = jnp.stack([partition_part, pos_part]).reshape(
        2, *[lax.axis_size(name) for name in layout], per_device
    )
    for name in layout:
        stats = sum_relative(stats, name, 1 + layout.index(name))
    stats = stats.reshape(2, -1)
    exponent_total = stats[0]
    matched_dot_value = stats[1]
    own_start = 0
    own_partition = lax.dynamic_slice_in_dim(exponent_total, own_start, per_device, 0)
    own_pos = lax.dynamic_slice_in_dim(matched_dot_value, own_start, per_device, 0)
    sample_loss = jnp.log(own_partition) - own_pos

    partial_sums = jnp.dot(weights, teacher_bank, preferred_element_type=jnp.float32)
    owned = (column == local_index[:, None]) & is_owner[:, None]
    owned_rows = jnp.dot(
        owned.astype(jnp.bfloat16), teacher_bank, preferred_element_type=jnp.float32
    )
    owned_inverse = jnp.sum(jnp.where(owned, inverse[None, :], 0.0), axis=1)
    local_owned_rows = owned_rows * owned_inverse[:, None]
    query_grad = (partial_sums / exponent_total[:, None] - local_owned_rows) / (
        sharpening_divisor * objective_divisor
    )
    query_grad = scatter_relative(query_grad, "bc")
    query_grad = scatter_two_ways(query_grad, scatter_relative, "bz", "bx")

    projection_gradient = (
        (query_grad - query * jnp.sum(query * query_grad, axis=1, keepdims=True)) / length
    ).astype(jnp.bfloat16)
    sizes = [lax.axis_size(name) for name in BANK_AXES]
    bank_size = sizes[0] * sizes[1] * sizes[2]
    order = [BANK_AXES.index(name) for name in reversed(GATHER_ORDER)]
    block_of = np.arange(bank_size).reshape(sizes).transpose(order).reshape(bank_size)
    in_share_rows = C_IN // bank_size
    head_share_rows = H // bank_size
    head_rows = (block_of[:, None] * head_share_rows + np.arange(head_share_rows)).reshape(-1)
    in_rows = (block_of[:, None] * in_share_rows + np.arange(in_share_rows)).reshape(-1)
    head_weight_piece = jnp.dot(
        spike_train_reduced[:, head_rows].T, projection_gradient, preferred_element_type=jnp.float32
    )
    spike_train_gradient = jnp.dot(
        projection_gradient, embedding_head_weight.T, preferred_element_type=jnp.float32
    )
    (input_current_gradient,) = leaky_neuron_backward(spike_train_gradient)
    current_low = input_current_gradient.astype(jnp.bfloat16).reshape(per_device * TIME, H)
    in_part = jnp.dot(flat_in[:, in_rows].T, current_low, preferred_element_type=jnp.float32)

    grads = jnp.concatenate(
        [
            in_part.reshape(bank_size, in_share_rows * H),
            head_weight_piece.reshape(bank_size, head_share_rows * D),
        ],
        axis=1,
    )
    grads = scatter_absolute(grads, "bc")
    grads = scatter_two_ways(grads, scatter_absolute, "bz", "bx")
    grads = sum_all(grads, "dp")
    in_grad = grads[0, : in_share_rows * H].reshape(in_share_rows, H)
    head_weight_gradient = grads[0, in_share_rows * H :].reshape(head_share_rows, D)
    return (sample_loss, in_grad, head_weight_gradient)


def split_mesh(mesh):
    devices = mesh.devices
    column = devices[:, 0]
    try:
        xs = sorted({int(d.coords[0]) for d in column})
        zs = sorted({int(d.coords[2]) for d in column})
        cs = sorted({int(d.core_on_chip) for d in column})
        nx, nz, nc = len(xs), len(zs), len(cs)
        ok = nx * nz * nc == column.shape[0]
        for b, d in enumerate(column):
            want = (b // (nz * nc), (b // nc) % nz, b % nc)
            got = (xs.index(int(d.coords[0])), zs.index(int(d.coords[2])), cs.index(int(d.core_on_chip)))
            ok = ok and want == got
    except (AttributeError, IndexError, TypeError):
        ok = False
    if not ok:
        nx, nz, nc = 1, 1, column.shape[0]
    return Mesh(devices.reshape(nx, nz, nc, devices.shape[1]), SAMPLE_AXES)


def solution(mesh):
    split = split_mesh(mesh)
    in_specs = (
        P(SAMPLE_AXES, None, None),
        P(SAMPLE_AXES, None),
        P(SAMPLE_AXES),
        P(BANK_AXES, None),
        P(),
        P(),
        P(),
    )
    out_specs = (P(SAMPLE_AXES), P(BANK_AXES, None), P(BANK_AXES, None))
    return jax.shard_map(body, mesh=split, in_specs=in_specs, out_specs=out_specs, check_vma=False)
```

```python
from functools import partial

import jax
import numpy as np
import jax.numpy as jnp
from jax import lax
from jax.sharding import Mesh
from jax.sharding import PartitionSpec as P

D = 1024
H = 512
C_IN = 128
TIME = 8


sharpening_divisor = 0.07
objective_divisor = 64.0
threshold = 1.0
sharpness = 4.0
epsilon = 1e-06

BANK_AXES = ("bx", "bz", "bc")
SAMPLE_AXES = ("bx", "bz", "bc", "dp")
GATHER_ORDER = ("bx", "bz", "bc")
CODE_COLS = 128


def membrane_potential(input_current, membrane_decay_rate):
    potential = jnp.zeros((input_current.shape[0], input_current.shape[2]), jnp.float32)
    spikes = jnp.zeros_like(potential)
    totals = jnp.zeros_like(potential)
    for moment in range(input_current.shape[1]):
        potential = membrane_decay_rate * potential + input_current[:, moment, :] - spikes
        spikes = jax.nn.sigmoid(sharpness * (potential - threshold))
        totals = totals + spikes
    return totals / input_current.shape[1]


def shift_pairs(name, shift):
    size = lax.axis_size(name)
    return [(j, (j + shift) % size) for j in range(size)]


def gather_relative(x, name):
    size = lax.axis_size(name)
    blocks = [x] + [lax.ppermute(x, name, shift_pairs(name, k)) for k in range(1, size)]
    return jnp.concatenate(blocks, axis=0)


def sum_relative(x, name, axis):
    size = lax.axis_size(name)
    total = x
    for k in range(1, size):
        total = total + jnp.roll(lax.ppermute(x, name, shift_pairs(name, k)), k, axis=axis)
    return total


def sum_all(x, name):
    size = lax.axis_size(name)
    total = x
    for k in range(1, size):
        total = total + lax.ppermute(x, name, shift_pairs(name, k))
    return total


def ring_scatter_sum(pick, name, size):
    total = pick(0)
    for k in range(1, size):
        total = total + lax.ppermute(pick(k), name, shift_pairs(name, -k))
    return total


def scatter_relative(x, name):
    size = lax.axis_size(name)
    blocks = x.reshape(size, x.shape[0] // size, *x.shape[1:])
    return ring_scatter_sum(lambda k: blocks[k], name, size)


def scatter_absolute(x, name):
    size = lax.axis_size(name)
    rows = x.shape[0] // size
    me = lax.axis_index(name)

    def pick(k):
        return lax.dynamic_slice_in_dim(x, ((me - k) % size) * rows, rows, 0)

    return ring_scatter_sum(pick, name, size)


def scatter_two_ways(x, scatter, first, second):
    n_first = lax.axis_size(first)
    n_second = lax.axis_size(second)
    half = x.shape[1] // 2
    one = scatter(scatter(x[:, :half], first), second)
    other = (
        x[:, half:]
        .reshape(n_first, n_second, -1, half)
        .transpose(1, 0, 2, 3)
        .reshape(x.shape[0], half)
    )
    other = scatter(scatter(other, second), first)
    return jnp.concatenate([one, other], axis=1)


def bank_index():
    index = 0
    for name in BANK_AXES:
        index = index * lax.axis_size(name) + lax.axis_index(name)
    return index


def body(
    event_features,
    event_bins,
    positive,
    teacher_bank,
    in_weight,
    embedding_head_weight,
    membrane_decay_rate,
):
    per_device = positive.shape[0]
    bank_rows = teacher_bank.shape[0]
    onehot = (event_bins[:, None, :] == jnp.arange(TIME, dtype=jnp.int32)[None, :, None]).astype(
        jnp.bfloat16
    )
    binned = jnp.einsum(
        "ste,sec->stc", onehot, event_features, preferred_element_type=jnp.float32
    ).astype(jnp.bfloat16)
    flat_in = binned.reshape(per_device * TIME, C_IN)
    input_current = jnp.dot(flat_in, in_weight, preferred_element_type=jnp.float32).reshape(
        per_device, TIME, H
    )
    spike_train, leaky_neuron_backward = jax.vjp(
        partial(membrane_potential, membrane_decay_rate=membrane_decay_rate), input_current
    )
    spike_train_reduced = spike_train.astype(jnp.bfloat16)
    projected_embedding = jnp.dot(
        spike_train_reduced, embedding_head_weight, preferred_element_type=jnp.float32
    )
    length = jnp.sqrt(
        jnp.sum(projected_embedding * projected_embedding, axis=1, keepdims=True) + epsilon
    )
    query = projected_embedding / length
    query_low = query.astype(jnp.bfloat16)

    digits = jnp.stack([(positive >> 12) & 63, (positive >> 6) & 63, positive & 63], axis=1)
    code = jnp.zeros((per_device, CODE_COLS), jnp.bfloat16).at[:, :3].set(
        digits.astype(jnp.bfloat16)
    )
    gathered = jnp.concatenate([query_low, code], axis=1)
    for name in GATHER_ORDER:
        gathered = gather_relative(gathered, name)
    gathered_query = gathered[:, :D]
    gathered_digits = gathered[:, D : D + 3].astype(jnp.int32)
    gathered_pos = (
        gathered_digits[:, 0] * 4096 + gathered_digits[:, 1] * 64 + gathered_digits[:, 2]
    )

    start_row = bank_index() * bank_rows
    inverse = 1.0 / jnp.sqrt(
        jnp.sum(jnp.square(teacher_bank.astype(jnp.float32)), axis=1) + epsilon
    )
    local_index = gathered_pos - start_row
    is_owner = (local_index >= 0) & (local_index < bank_rows)
    local_index = jnp.clip(local_index, 0, bank_rows - 1)

    cosine_affinity_matrix = (
        jnp.dot(gathered_query, teacher_bank.T, preferred_element_type=jnp.float32)
        * inverse[None, :]
        / sharpening_divisor
    )
    exponent = jnp.exp(cosine_affinity_matrix)
    weights = (exponent * inverse[None, :]).astype(jnp.bfloat16)
    partition_part = jnp.sum(exponent, axis=1)
    column = lax.broadcasted_iota(jnp.int32, cosine_affinity_matrix.shape, 1)
    picked = jnp.sum(
        jnp.where(column == local_index[:, None], cosine_affinity_matrix, 0.0), axis=1
    )
    pos_part = jnp.where(is_owner, picked, 0.0)

    layout = list(reversed(GATHER_ORDER))
    stats = jnp.stack([partition_part, pos_part]).reshape(
        2, *[lax.axis_size(name) for name in layout], per_device
    )
    for name in layout:
        stats = sum_relative(stats, name, 1 + layout.index(name))
    stats = stats.reshape(2, -1)
    exponent_total = stats[0]
    matched_dot_value = stats[1]
    own_start = 0
    own_partition = lax.dynamic_slice_in_dim(exponent_total, own_start, per_device, 0)
    own_pos = lax.dynamic_slice_in_dim(matched_dot_value, own_start, per_device, 0)
    sample_loss = jnp.log(own_partition) - own_pos

    owned = (column == local_index[:, None]) & is_owner[:, None]
    both = jnp.dot(
        jnp.concatenate([weights, owned.astype(jnp.bfloat16)], axis=0),
        teacher_bank,
        preferred_element_type=jnp.float32,
    )
    partial_sums = both[: weights.shape[0]]
    owned_rows = both[weights.shape[0] :]
    owned_inverse = jnp.sum(jnp.where(owned, inverse[None, :], 0.0), axis=1)
    local_owned_rows = owned_rows * owned_inverse[:, None]
    query_grad = (partial_sums / exponent_total[:, None] - local_owned_rows) / (
        sharpening_divisor * objective_divisor
    )
    query_grad = scatter_relative(query_grad, "bc")
    query_grad = scatter_two_ways(query_grad, scatter_relative, "bz", "bx")

    projection_gradient = (
        (query_grad - query * jnp.sum(query * query_grad, axis=1, keepdims=True)) / length
    ).astype(jnp.bfloat16)
    sizes = [lax.axis_size(name) for name in BANK_AXES]
    bank_size = sizes[0] * sizes[1] * sizes[2]
    order = [BANK_AXES.index(name) for name in reversed(GATHER_ORDER)]
    block_of = np.arange(bank_size).reshape(sizes).transpose(order).reshape(bank_size)
    in_share_rows = C_IN // bank_size
    head_share_rows = H // bank_size
    head_rows = (block_of[:, None] * head_share_rows + np.arange(head_share_rows)).reshape(-1)
    in_rows = (block_of[:, None] * in_share_rows + np.arange(in_share_rows)).reshape(-1)
    head_weight_piece = jnp.dot(
        spike_train_reduced[:, head_rows].T, projection_gradient, preferred_element_type=jnp.float32
    )
    spike_train_gradient = jnp.dot(
        projection_gradient, embedding_head_weight.T, preferred_element_type=jnp.float32
    )
    (input_current_gradient,) = leaky_neuron_backward(spike_train_gradient)
    current_low = input_current_gradient.astype(jnp.bfloat16).reshape(per_device * TIME, H)
    in_part = jnp.dot(flat_in[:, in_rows].T, current_low, preferred_element_type=jnp.float32)

    grads = jnp.concatenate(
        [
            in_part.reshape(bank_size, in_share_rows * H),
            head_weight_piece.reshape(bank_size, head_share_rows * D),
        ],
        axis=1,
    )
    grads = scatter_absolute(grads, "bc")
    grads = scatter_two_ways(grads, scatter_absolute, "bz", "bx")
    grads = sum_all(grads, "dp")
    in_grad = grads[0, : in_share_rows * H].reshape(in_share_rows, H)
    head_weight_gradient = grads[0, in_share_rows * H :].reshape(head_share_rows, D)
    return (sample_loss, in_grad, head_weight_gradient)


def split_mesh(mesh):
    devices = mesh.devices
    column = devices[:, 0]
    try:
        xs = sorted({int(d.coords[0]) for d in column})
        zs = sorted({int(d.coords[2]) for d in column})
        cs = sorted({int(d.core_on_chip) for d in column})
        nx, nz, nc = len(xs), len(zs), len(cs)
        ok = nx * nz * nc == column.shape[0]
        for b, d in enumerate(column):
            want = (b // (nz * nc), (b // nc) % nz, b % nc)
            got = (xs.index(int(d.coords[0])), zs.index(int(d.coords[2])), cs.index(int(d.core_on_chip)))
            ok = ok and want == got
    except (AttributeError, IndexError, TypeError):
        ok = False
    if not ok:
        nx, nz, nc = 1, 1, column.shape[0]
    return Mesh(devices.reshape(nx, nz, nc, devices.shape[1]), SAMPLE_AXES)


def solution(mesh):
    split = split_mesh(mesh)
    in_specs = (
        P(SAMPLE_AXES, None, None),
        P(SAMPLE_AXES, None),
        P(SAMPLE_AXES),
        P(BANK_AXES, None),
        P(),
        P(),
        P(),
    )
    out_specs = (P(SAMPLE_AXES), P(BANK_AXES, None), P(BANK_AXES, None))
    return jax.shard_map(body, mesh=split, in_specs=in_specs, out_specs=out_specs, check_vma=False)
```

```python
from functools import partial

import jax
import numpy as np
import jax.numpy as jnp
from jax import lax
from jax.sharding import Mesh
from jax.sharding import PartitionSpec as P

D = 1024
H = 512
C_IN = 128
TIME = 8


sharpening_divisor = 0.07
objective_divisor = 64.0
threshold = 1.0
sharpness = 4.0
epsilon = 1e-06

BANK_AXES = ("bx", "bz", "bc")
SAMPLE_AXES = ("bx", "bz", "bc", "dp")
GATHER_ORDER = ("bx", "bz", "bc")
CODE_COLS = 128


def membrane_potential(input_current, membrane_decay_rate):
    potential = jnp.zeros((input_current.shape[0], input_current.shape[2]), jnp.float32)
    spikes = jnp.zeros_like(potential)
    totals = jnp.zeros_like(potential)
    for moment in range(input_current.shape[1]):
        potential = membrane_decay_rate * potential + input_current[:, moment, :] - spikes
        spikes = jax.nn.sigmoid(sharpness * (potential - threshold))
        totals = totals + spikes
    return totals / input_current.shape[1]


def shift_pairs(name, shift):
    size = lax.axis_size(name)
    return [(j, (j + shift) % size) for j in range(size)]


def gather_relative(x, name):
    size = lax.axis_size(name)
    blocks = [x] + [lax.ppermute(x, name, shift_pairs(name, k)) for k in range(1, size)]
    return jnp.concatenate(blocks, axis=0)


def sum_relative(x, name, axis):
    size = lax.axis_size(name)
    total = x
    for k in range(1, size):
        total = total + jnp.roll(lax.ppermute(x, name, shift_pairs(name, k)), k, axis=axis)
    return total


def sum_all(x, name):
    size = lax.axis_size(name)
    total = x
    for k in range(1, size):
        total = total + lax.ppermute(x, name, shift_pairs(name, k))
    return total


def ring_scatter_sum(pick, name, size):
    total = pick(0)
    for k in range(1, size):
        total = total + lax.ppermute(pick(k), name, shift_pairs(name, -k))
    return total


def scatter_relative(x, name):
    size = lax.axis_size(name)
    blocks = x.reshape(size, x.shape[0] // size, *x.shape[1:])
    return ring_scatter_sum(lambda k: blocks[k], name, size)


def scatter_absolute(x, name):
    size = lax.axis_size(name)
    rows = x.shape[0] // size
    me = lax.axis_index(name)

    def pick(k):
        return lax.dynamic_slice_in_dim(x, ((me - k) % size) * rows, rows, 0)

    return ring_scatter_sum(pick, name, size)


def scatter_two_ways(x, scatter, first, second):
    n_first = lax.axis_size(first)
    n_second = lax.axis_size(second)
    half = max(128, int(round(x.shape[1] / 3 / 128)) * 128)
    one = scatter(scatter(x[:, :half], first), second)
    other = (
        x[:, half:]
        .reshape(n_first, n_second, -1, x.shape[1] - half)
        .transpose(1, 0, 2, 3)
        .reshape(x.shape[0], x.shape[1] - half)
    )
    other = scatter(scatter(other, second), first)
    return jnp.concatenate([one, other], axis=1)


def bank_index():
    index = 0
    for name in BANK_AXES:
        index = index * lax.axis_size(name) + lax.axis_index(name)
    return index


def body(
    event_features,
    event_bins,
    positive,
    teacher_bank,
    in_weight,
    embedding_head_weight,
    membrane_decay_rate,
):
    per_device = positive.shape[0]
    bank_rows = teacher_bank.shape[0]
    onehot = (event_bins[:, None, :] == jnp.arange(TIME, dtype=jnp.int32)[None, :, None]).astype(
        jnp.bfloat16
    )
    binned = jnp.einsum(
        "ste,sec->stc", onehot, event_features, preferred_element_type=jnp.float32
    ).astype(jnp.bfloat16)
    flat_in = binned.reshape(per_device * TIME, C_IN)
    input_current = jnp.dot(flat_in, in_weight, preferred_element_type=jnp.float32).reshape(
        per_device, TIME, H
    )
    spike_train, leaky_neuron_backward = jax.vjp(
        partial(membrane_potential, membrane_decay_rate=membrane_decay_rate), input_current
    )
    spike_train_reduced = spike_train.astype(jnp.bfloat16)
    projected_embedding = jnp.dot(
        spike_train_reduced, embedding_head_weight, preferred_element_type=jnp.float32
    )
    length = jnp.sqrt(
        jnp.sum(projected_embedding * projected_embedding, axis=1, keepdims=True) + epsilon
    )
    query = projected_embedding / length
    query_low = query.astype(jnp.bfloat16)

    digits = jnp.stack([(positive >> 12) & 63, (positive >> 6) & 63, positive & 63], axis=1)
    code = jnp.zeros((per_device, CODE_COLS), jnp.bfloat16).at[:, :3].set(
        digits.astype(jnp.bfloat16)
    )
    gathered = jnp.concatenate([query_low, code], axis=1)
    for name in GATHER_ORDER:
        gathered = gather_relative(gathered, name)
    gathered_query = gathered[:, :D]
    gathered_digits = gathered[:, D : D + 3].astype(jnp.int32)
    gathered_pos = (
        gathered_digits[:, 0] * 4096 + gathered_digits[:, 1] * 64 + gathered_digits[:, 2]
    )

    start_row = bank_index() * bank_rows
    inverse = 1.0 / jnp.sqrt(
        jnp.sum(jnp.square(teacher_bank.astype(jnp.float32)), axis=1) + epsilon
    )
    local_index = gathered_pos - start_row
    is_owner = (local_index >= 0) & (local_index < bank_rows)
    local_index = jnp.clip(local_index, 0, bank_rows - 1)

    cosine_affinity_matrix = (
        jnp.dot(gathered_query, teacher_bank.T, preferred_element_type=jnp.float32)
        * inverse[None, :]
        / sharpening_divisor
    )
    exponent = jnp.exp(cosine_affinity_matrix)
    weights = (exponent * inverse[None, :]).astype(jnp.bfloat16)
    partition_part = jnp.sum(exponent, axis=1)
    column = lax.broadcasted_iota(jnp.int32, cosine_affinity_matrix.shape, 1)
    picked = jnp.sum(
        jnp.where(column == local_index[:, None], cosine_affinity_matrix, 0.0), axis=1
    )
    pos_part = jnp.where(is_owner, picked, 0.0)

    layout = list(reversed(GATHER_ORDER))
    stats = jnp.stack([partition_part, pos_part]).reshape(
        2, *[lax.axis_size(name) for name in layout], per_device
    )
    for name in layout:
        stats = sum_relative(stats, name, 1 + layout.index(name))
    stats = stats.reshape(2, -1)
    exponent_total = stats[0]
    matched_dot_value = stats[1]
    own_start = 0
    own_partition = lax.dynamic_slice_in_dim(exponent_total, own_start, per_device, 0)
    own_pos = lax.dynamic_slice_in_dim(matched_dot_value, own_start, per_device, 0)
    sample_loss = jnp.log(own_partition) - own_pos

    owned = (column == local_index[:, None]) & is_owner[:, None]
    both = jnp.dot(
        jnp.concatenate([weights, owned.astype(jnp.bfloat16)], axis=0),
        teacher_bank,
        preferred_element_type=jnp.float32,
    )
    partial_sums = both[: weights.shape[0]]
    owned_rows = both[weights.shape[0] :]
    owned_inverse = jnp.sum(jnp.where(owned, inverse[None, :], 0.0), axis=1)
    local_owned_rows = owned_rows * owned_inverse[:, None]
    query_grad = (partial_sums / exponent_total[:, None] - local_owned_rows) / (
        sharpening_divisor * objective_divisor
    )
    query_grad = scatter_relative(query_grad, "bc")
    query_grad = scatter_two_ways(query_grad, scatter_relative, "bz", "bx")

    projection_gradient = (
        (query_grad - query * jnp.sum(query * query_grad, axis=1, keepdims=True)) / length
    ).astype(jnp.bfloat16)
    sizes = [lax.axis_size(name) for name in BANK_AXES]
    bank_size = sizes[0] * sizes[1] * sizes[2]
    order = [BANK_AXES.index(name) for name in reversed(GATHER_ORDER)]
    block_of = np.arange(bank_size).reshape(sizes).transpose(order).reshape(bank_size)
    in_share_rows = C_IN // bank_size
    head_share_rows = H // bank_size
    head_rows = (block_of[:, None] * head_share_rows + np.arange(head_share_rows)).reshape(-1)
    in_rows = (block_of[:, None] * in_share_rows + np.arange(in_share_rows)).reshape(-1)
    head_weight_piece = jnp.dot(
        spike_train_reduced[:, head_rows].T, projection_gradient, preferred_element_type=jnp.float32
    )
    spike_train_gradient = jnp.dot(
        projection_gradient, embedding_head_weight.T, preferred_element_type=jnp.float32
    )
    (input_current_gradient,) = leaky_neuron_backward(spike_train_gradient)
    current_low = input_current_gradient.astype(jnp.bfloat16).reshape(per_device * TIME, H)
    in_part = jnp.dot(flat_in[:, in_rows].T, current_low, preferred_element_type=jnp.float32)

    grads = jnp.concatenate(
        [
            in_part.reshape(bank_size, in_share_rows * H),
            head_weight_piece.reshape(bank_size, head_share_rows * D),
        ],
        axis=1,
    )
    grads = scatter_absolute(grads, "bc")
    grads = scatter_two_ways(grads, scatter_absolute, "bz", "bx")
    grads = sum_all(grads, "dp")
    in_grad = grads[0, : in_share_rows * H].reshape(in_share_rows, H)
    head_weight_gradient = grads[0, in_share_rows * H :].reshape(head_share_rows, D)
    return (sample_loss, in_grad, head_weight_gradient)


def split_mesh(mesh):
    devices = mesh.devices
    column = devices[:, 0]
    try:
        xs = sorted({int(d.coords[0]) for d in column})
        zs = sorted({int(d.coords[2]) for d in column})
        cs = sorted({int(d.core_on_chip) for d in column})
        nx, nz, nc = len(xs), len(zs), len(cs)
        ok = nx * nz * nc == column.shape[0]
        for b, d in enumerate(column):
            want = (b // (nz * nc), (b // nc) % nz, b % nc)
            got = (xs.index(int(d.coords[0])), zs.index(int(d.coords[2])), cs.index(int(d.core_on_chip)))
            ok = ok and want == got
    except (AttributeError, IndexError, TypeError):
        ok = False
    if not ok:
        nx, nz, nc = 1, 1, column.shape[0]
    return Mesh(devices.reshape(nx, nz, nc, devices.shape[1]), SAMPLE_AXES)


def solution(mesh):
    split = split_mesh(mesh)
    in_specs = (
        P(SAMPLE_AXES, None, None),
        P(SAMPLE_AXES, None),
        P(SAMPLE_AXES),
        P(BANK_AXES, None),
        P(),
        P(),
        P(),
    )
    out_specs = (P(SAMPLE_AXES), P(BANK_AXES, None), P(BANK_AXES, None))
    return jax.shard_map(body, mesh=split, in_specs=in_specs, out_specs=out_specs, check_vma=False)
```
